32 devices in a mesh: rep: 4 (over x, core), dev: 8 (over z, y).
Axes of the slice: x: 2, y: 2, z: 4, core: 2. Of those that a mesh axis runs over, the one named last changes fastest.
Arguments:
- group_weights: bfloat16 [4, 160, 128, 1024], P('rep', None, 'dev'), may hold values from -6 to 6
- owner: int32 [160], replicated, may hold values from 0 to 7, as said below
- start_weights: float32 [8, 40, 128, 1024], P('dev', None, None, 'rep'), may hold values from -6 to 6
- momentum: float32 [8, 40, 128, 1024], P('dev', None, None, 'rep'), may hold values from -6 to 6
- basis: float32 [64, 1024], replicated, may hold values from -1 to 1
- vec_groups: bfloat16 [4, 13, 1024], P('rep'), may hold values from -6 to 6
- vec_start: float32 [13, 1024], replicated, may hold values from -6 to 6
- vec_momentum: float32 [13, 1024], replicated, may hold values from -6 to 6
Outputs:
- new_start: float32 [8, 40, 128, 1024], P('dev', None, None, 'rep')
- new_momentum: float32 [8, 40, 128, 1024], P('dev', None, None, 'rep')
- returned: bfloat16 [160, 128, 1024], P(None, 'dev')
- vec_new: float32 [13, 1024], replicated
- vec_new_momentum: float32 [13, 1024], replicated
The draws below stay inside these ranges and needn't reach their ends.
Inputs may be any that keep to these rules, and one draw needn't show every extreme that they name: `owner`: each index along dev owns at most 40 blocks, and some index owns exactly 40.
All inputs are finite; a program needn't handle non-finite values.
Results may differ from the reference program's by a relative error of at most 0.012.
Values may be sent and summed in bfloat16 or wider, within the bound.
No kernel may reach another device: no remote copies, remote signals or barrier semaphores. Data moves between devices by JAX's collectives and lax.ppermute only.
A program may use at most 128 MiB of HBM per device.

```python
import jax
import jax.numpy as jnp
from jax import lax

D = 1024
RANK = 64
BLOCK = 128
UNITS = 160
EMB_FIRST = 96
SLOTS = 40
NVEC = 13
N_REP = 4
N_DEV = 8


def draw_owner(key, part):
    key_full, key_spread, key_order = jax.random.split(key, 3)
    busiest = jax.random.randint(key_full, (), 0, N_DEV, dtype=jnp.int32)
    spread = jax.random.permutation(key_spread, (N_DEV - 1) * SLOTS)[:UNITS - SLOTS] // SLOTS
    spread = spread.astype(jnp.int32)
    spread = spread + (spread >= busiest).astype(jnp.int32)
    owners = jnp.concatenate([jnp.ones((SLOTS,), jnp.int32) * busiest, spread])
    return jnp.take(owners, jax.random.permutation(key_order, UNITS)).astype(jnp.int32)


def shard_levels(own_key, extent, cuts, smallest, top_value):
    def one(position, blocks):
        steps = jax.random.uniform(jax.random.fold_in(jax.random.fold_in(own_key, 6), position), (blocks,), jnp.float32, smallest / len(cuts), top_value / len(cuts))
        return jnp.repeat(jnp.exp(steps), extent[position] // blocks).reshape((-1,) + (1,) * (len(extent) - position - 1))

    level = one(*cuts[0])
    for cut in cuts[1:]:
        level = level * one(*cut)
    return level


def noise(stream_key, extent, scale, limit, cuts=(), held_as=jnp.bfloat16):
    loudness = shard_levels(stream_key, extent, cuts, -0.22, 0.18) if cuts else 1.0
    values = jax.random.normal(stream_key, extent, jnp.float32) * scale * loudness
    return jnp.minimum(jnp.maximum(values, -limit), limit).astype(held_as)


def setup_inputs(seed: int = 0) -> dict:
    key_of = jax.random.split(jax.random.key(seed), 9)
    group_weights = noise(key_of[0], (N_REP, UNITS, BLOCK, D), 1.0, 6.0, ((0, 4), (2, 8)))
    owner = draw_owner(jax.random.fold_in(key_of[8], 71), 0)
    start_weights = noise(key_of[2], (N_DEV, SLOTS, BLOCK, D), 1.0, 6.0, ((0, 8), (3, 4)), jnp.float32)
    momentum = noise(key_of[3], (N_DEV, SLOTS, BLOCK, D), 0.5, 6.0, ((0, 8), (3, 4)), jnp.float32)
    basis = noise(key_of[4], (RANK, D), 0.0625, 1.0, (), jnp.float32)
    vec_groups = noise(key_of[5], (N_REP, NVEC, D), 1.0, 6.0, ((0, 4),))
    vec_start = noise(key_of[6], (NVEC, D), 1.0, 6.0, (), jnp.float32)
    vec_momentum = noise(key_of[7], (NVEC, D), 0.5, 6.0, (), jnp.float32)
    return dict(group_weights=group_weights, owner=owner, start_weights=start_weights, momentum=momentum, basis=basis, vec_groups=vec_groups, vec_start=vec_start, vec_momentum=vec_momentum)


outer_rate = 0.7
outer_momentum = 0.9


def reference(group_weights, owner, start_weights, momentum, basis, vec_groups, vec_start, vec_momentum):
    unit_ids = jnp.arange(UNITS, dtype=jnp.int32)
    same_owner = owner[:, None] == owner[None, :]
    earlier = unit_ids[None, :] < unit_ids[:, None]
    slot_of = jnp.sum((same_owner & earlier).astype(jnp.int32), axis=1).astype(jnp.int32)
    group_mean = jnp.sum(group_weights.astype(jnp.float32), axis=0) / N_REP
    start_rows = start_weights[owner, slot_of]
    momentum_rows = momentum[owner, slot_of]
    change = start_rows - group_mean
    coeffs = jnp.einsum("ubd,kd->ubk", change, basis, precision=lax.Precision.HIGHEST)
    projected = jnp.einsum("ubk,kd->ubd", coeffs, basis, precision=lax.Precision.HIGHEST)
    is_embedding = (unit_ids >= EMB_FIRST)[:, None, None]
    outer_grad = jnp.where(is_embedding, projected, change)
    fresh_momentum = outer_momentum * momentum_rows + outer_grad
    fresh_start = start_rows - outer_rate * (outer_grad + outer_momentum * fresh_momentum)
    new_start = start_weights.at[owner, slot_of].set(fresh_start)
    new_momentum = momentum.at[owner, slot_of].set(fresh_momentum)
    returned = fresh_start.astype(jnp.bfloat16)
    vec_change = vec_start - jnp.sum(vec_groups.astype(jnp.float32), axis=0) / N_REP
    vec_new_momentum = outer_momentum * vec_momentum + vec_change
    vec_new = vec_start - outer_rate * (vec_change + outer_momentum * vec_new_momentum)
    return new_start, new_momentum, returned, vec_new, vec_new_momentum
```

```python
import jax
import jax.numpy as jnp
from jax import lax
from jax.sharding import PartitionSpec as P

EMB_FIRST = 96


outer_rate = 0.7
outer_momentum = 0.9


def body(group_weights, owner, start_weights, momentum, basis, vec_groups, vec_start, vec_momentum):
    dev_count = lax.axis_size("dev")
    rep_count = lax.axis_size("rep")
    unit_count = owner.shape[0]
    slot_count = start_weights.shape[1]
    quarter = start_weights.shape[3]
    unit_ids = jnp.arange(unit_count, dtype=jnp.int32)
    same_owner = owner[:, None] == owner[None, :]
    earlier = unit_ids[None, :] < unit_ids[:, None]
    slot_of = jnp.sum((same_owner & earlier).astype(jnp.int32), axis=1)
    target = owner * slot_count + slot_of
    positions = jnp.arange(dev_count * slot_count, dtype=jnp.int32)
    placed = target[:, None] == positions[None, :]
    source_unit = jnp.sum(jnp.where(placed, unit_ids[:, None], 0), axis=0)
    own_rows = group_weights[0]
    summed = lax.psum_scatter(own_rows, "rep", scatter_dimension=2, tiled=True)
    picked = jnp.take(summed, source_unit, axis=0)
    arrived = lax.all_to_all(
        picked.reshape(dev_count, slot_count, summed.shape[1], summed.shape[2]),
        "dev",
        split_axis=0,
        concat_axis=2,
        tiled=True,
    )
    group_mean = arrived[0].astype(jnp.float32) / rep_count
    start_rows = start_weights[0]
    momentum_rows = momentum[0]
    my_slots = lax.axis_index("dev") * slot_count + jnp.arange(slot_count, dtype=jnp.int32)
    own_placed = target[:, None] == my_slots[None, :]
    is_owned = jnp.any(own_placed, axis=0)
    is_embedding = jnp.any(own_placed & (unit_ids >= EMB_FIRST)[:, None], axis=0)
    change = start_rows - group_mean
    first_column = lax.axis_index("rep") * quarter
    basis_part = lax.dynamic_slice_in_dim(basis, first_column, quarter, 1)
    coeff_terms = jnp.einsum("sbq,kq->sbk", change, basis_part, precision=lax.Precision.HIGHEST)
    vec_terms = vec_groups[0]
    coeff_flat = coeff_terms.astype(jnp.bfloat16).reshape(-1)
    joined = lax.psum(jnp.concatenate([coeff_flat, vec_terms.reshape(-1)]), "rep")
    coeffs = joined[: coeff_flat.shape[0]].reshape(coeff_terms.shape).astype(jnp.float32)
    vec_summed = joined[coeff_flat.shape[0]:].reshape(vec_terms.shape).astype(jnp.float32)
    projected = jnp.einsum("sbk,kq->sbq", coeffs, basis_part, precision=lax.Precision.HIGHEST)
    outer_grad = jnp.where(is_embedding[:, None, None], projected, change)
    fresh_momentum = outer_momentum * momentum_rows + outer_grad
    fresh_start = start_rows - outer_rate * (outer_grad + outer_momentum * fresh_momentum)
    owned_mask = is_owned[:, None, None]
    new_momentum = jnp.where(owned_mask, fresh_momentum, momentum_rows)
    new_start = jnp.where(owned_mask, fresh_start, start_rows)
    rounded = fresh_start.astype(jnp.bfloat16)
    pieces = lax.all_to_all(rounded, "dev", split_axis=1, concat_axis=0, tiled=True)
    picked = jnp.take(pieces, target, axis=0)
    returned = lax.all_gather(picked, "rep", axis=2, tiled=True)
    vec_change = vec_start - vec_summed / rep_count
    vec_new_momentum = outer_momentum * vec_momentum + vec_change
    vec_new = vec_start - outer_rate * (vec_change + outer_momentum * vec_new_momentum)
    return (new_start[None], new_momentum[None], returned, vec_new, vec_new_momentum)


def solution(mesh):
    return jax.shard_map(
        body,
        mesh=mesh,
        in_specs=(
            P("rep", None, "dev", None),
            P(),
            P("dev", None, None, "rep"),
            P("dev", None, None, "rep"),
            P(),
            P("rep", None, None),
            P(),
            P(),
        ),
        out_specs=(
            P("dev", None, None, "rep"),
            P("dev", None, None, "rep"),
            P(None, "dev", None),
            P(),
            P(),
        ),
        check_vma=False,
    )
```

```python
import jax
import jax.numpy as jnp
from jax import lax
from jax.sharding import PartitionSpec as P

EMB_FIRST = 96
CHUNKS = 2


outer_rate = 0.7
outer_momentum = 0.9


def body(group_weights, owner, start_weights, momentum, basis, vec_groups, vec_start, vec_momentum):
    dev_count = lax.axis_size("dev")
    rep_count = lax.axis_size("rep")
    unit_count = owner.shape[0]
    slot_count = start_weights.shape[1]
    quarter = start_weights.shape[3]
    width = quarter // CHUNKS
    unit_ids = jnp.arange(unit_count, dtype=jnp.int32)
    same_owner = owner[:, None] == owner[None, :]
    earlier = unit_ids[None, :] < unit_ids[:, None]
    slot_of = jnp.sum((same_owner & earlier).astype(jnp.int32), axis=1)
    target = owner * slot_count + slot_of
    positions = jnp.arange(dev_count * slot_count, dtype=jnp.int32)
    placed = target[:, None] == positions[None, :]
    source_unit = jnp.sum(jnp.where(placed, unit_ids[:, None], 0), axis=0)
    own_rows = group_weights[0]
    rows = own_rows.shape[1]
    split_rows = own_rows.reshape(unit_count, rows, rep_count, CHUNKS, width)
    start_rows = start_weights[0]
    momentum_rows = momentum[0]
    my_slots = lax.axis_index("dev") * slot_count + jnp.arange(slot_count, dtype=jnp.int32)
    own_placed = target[:, None] == my_slots[None, :]
    is_owned = jnp.any(own_placed, axis=0)
    is_embedding = jnp.any(own_placed & (unit_ids >= EMB_FIRST)[:, None], axis=0)
    first_column = lax.axis_index("rep") * quarter
    basis_part = lax.dynamic_slice_in_dim(basis, first_column, quarter, 1)

    changes = []
    coeff_terms = None
    for c in range(CHUNKS):
        chunk = split_rows[:, :, :, c, :].reshape(unit_count, rows, rep_count * width)
        summed = lax.psum_scatter(chunk, "rep", scatter_dimension=2, tiled=True)
        picked = jnp.take(summed, source_unit, axis=0, mode="clip")
        arrived = lax.all_to_all(
            picked.reshape(dev_count, slot_count, rows, width),
            "dev",
            split_axis=0,
            concat_axis=2,
            tiled=True,
        )
        group_mean = arrived[0].astype(jnp.float32) / rep_count
        change = start_rows[:, :, c * width:(c + 1) * width] - group_mean
        changes.append(change)
        term = jnp.einsum(
            "sbq,kq->sbk", change, basis_part[:, c * width:(c + 1) * width], precision=lax.Precision.HIGHEST
        )
        coeff_terms = term if coeff_terms is None else coeff_terms + term

    vec_terms = vec_groups[0].astype(jnp.float32)
    coeff_flat = coeff_terms.reshape(-1)
    joined = lax.psum(jnp.concatenate([coeff_flat, vec_terms.reshape(-1)]), "rep")
    coeffs = joined[: coeff_flat.shape[0]].reshape(coeff_terms.shape)
    vec_summed = joined[coeff_flat.shape[0]:].reshape(vec_terms.shape)

    owned_mask = is_owned[:, None, None]
    new_starts, new_momenta, returned_parts = [], [], []
    for c in range(CHUNKS):
        cols = slice(c * width, (c + 1) * width)
        projected = jnp.einsum("sbk,kq->sbq", coeffs, basis_part[:, cols], precision=lax.Precision.HIGHEST)
        outer_grad = jnp.where(is_embedding[:, None, None], projected, changes[c])
        fresh_momentum = outer_momentum * momentum_rows[:, :, cols] + outer_grad
        fresh_start = start_rows[:, :, cols] - outer_rate * (outer_grad + outer_momentum * fresh_momentum)
        new_momenta.append(jnp.where(owned_mask, fresh_momentum, momentum_rows[:, :, cols]))
        new_starts.append(jnp.where(owned_mask, fresh_start, start_rows[:, :, cols]))
        rounded = fresh_start.astype(jnp.bfloat16)
        pieces = lax.all_to_all(rounded, "dev", split_axis=1, concat_axis=0, tiled=True)
        picked = jnp.take(pieces, target, axis=0, mode="clip")
        returned_parts.append(lax.all_gather(picked[:, :, None, :], "rep", axis=2, tiled=True))
    returned = jnp.stack(returned_parts, axis=3).reshape(unit_count, rows, rep_count * quarter)
    new_start = jnp.concatenate(new_starts, axis=2)
    new_momentum = jnp.concatenate(new_momenta, axis=2)
    vec_change = vec_start - vec_summed / rep_count
    vec_new_momentum = outer_momentum * vec_momentum + vec_change
    vec_new = vec_start - outer_rate * (vec_change + outer_momentum * vec_new_momentum)
    return (new_start[None], new_momentum[None], returned, vec_new, vec_new_momentum)


def solution(mesh):
    return jax.shard_map(
        body,
        mesh=mesh,
        in_specs=(
            P("rep", None, "dev", None),
            P(),
            P("dev", None, None, "rep"),
            P("dev", None, None, "rep"),
            P(),
            P("rep", None, None),
            P(),
            P(),
        ),
        out_specs=(
            P("dev", None, None, "rep"),
            P("dev", None, None, "rep"),
            P(None, "dev", None),
            P(),
            P(),
        ),
        check_vma=False,
    )
```

```python
import jax
import jax.numpy as jnp
from jax import lax
from jax.sharding import PartitionSpec as P

EMB_FIRST = 96


outer_rate = 0.7
outer_momentum = 0.9


def rep_sum(x):
    rep_count = lax.axis_size("rep")
    total = x.astype(jnp.bfloat16)
    step = 1
    while step < rep_count:
        other = lax.ppermute(total, "rep", [(i, i ^ step) for i in range(rep_count)])
        total = total.astype(jnp.float32) + other.astype(jnp.float32)
        step *= 2
        if step < rep_count:
            total = total.astype(jnp.bfloat16)
    return total


def body(group_weights, owner, start_weights, momentum, basis, vec_groups, vec_start, vec_momentum):
    dev_count = lax.axis_size("dev")
    rep_count = lax.axis_size("rep")
    unit_count = owner.shape[0]
    slot_count = start_weights.shape[1]
    quarter = start_weights.shape[3]
    unit_ids = jnp.arange(unit_count, dtype=jnp.int32)
    same_owner = owner[:, None] == owner[None, :]
    earlier = unit_ids[None, :] < unit_ids[:, None]
    slot_of = jnp.sum((same_owner & earlier).astype(jnp.int32), axis=1)
    target = owner * slot_count + slot_of
    positions = jnp.arange(dev_count * slot_count, dtype=jnp.int32)
    placed = target[:, None] == positions[None, :]
    source_unit = jnp.sum(jnp.where(placed, unit_ids[:, None], 0), axis=0)
    own_rows = group_weights[0]
    summed = lax.psum_scatter(own_rows, "rep", scatter_dimension=2, tiled=True)
    picked = jnp.take(summed, source_unit, axis=0, mode="clip")
    arrived = lax.all_to_all(
        picked.reshape(dev_count, slot_count, summed.shape[1], summed.shape[2]),
        "dev",
        split_axis=0,
        concat_axis=2,
        tiled=True,
    )
    group_mean = arrived[0].astype(jnp.float32) / rep_count
    start_rows = start_weights[0]
    momentum_rows = momentum[0]
    my_slots = lax.axis_index("dev") * slot_count + jnp.arange(slot_count, dtype=jnp.int32)
    own_placed = target[:, None] == my_slots[None, :]
    is_owned = jnp.any(own_placed, axis=0)
    is_embedding = jnp.any(own_placed & (unit_ids >= EMB_FIRST)[:, None], axis=0)
    change = start_rows - group_mean
    first_column = lax.axis_index("rep") * quarter
    basis_part = lax.dynamic_slice_in_dim(basis, first_column, quarter, 1)
    coeff_terms = jnp.einsum("sbq,kq->sbk", change, basis_part, precision=lax.Precision.HIGHEST)
    vec_terms = vec_groups[0]
    coeff_flat = coeff_terms.astype(jnp.bfloat16).reshape(-1)
    joined = rep_sum(jnp.concatenate([coeff_flat, vec_terms.reshape(-1)]))
    coeffs = joined[: coeff_flat.shape[0]].reshape(coeff_terms.shape)
    vec_summed = joined[coeff_flat.shape[0]:].reshape(vec_terms.shape)
    projected = jnp.einsum("sbk,kq->sbq", coeffs, basis_part, precision=lax.Precision.HIGHEST)
    outer_grad = jnp.where(is_embedding[:, None, None], projected, change)
    fresh_momentum = outer_momentum * momentum_rows + outer_grad
    fresh_start = start_rows - outer_rate * (outer_grad + outer_momentum * fresh_momentum)
    owned_mask = is_owned[:, None, None]
    new_momentum = jnp.where(owned_mask, fresh_momentum, momentum_rows)
    new_start = jnp.where(owned_mask, fresh_start, start_rows)
    rounded = fresh_start.astype(jnp.bfloat16)
    pieces = lax.all_to_all(rounded, "dev", split_axis=1, concat_axis=0, tiled=True)
    picked = jnp.take(pieces, target, axis=0, mode="clip")
    returned = lax.all_gather(picked, "rep", axis=2, tiled=True)
    vec_change = vec_start - vec_summed / rep_count
    vec_new_momentum = outer_momentum * vec_momentum + vec_change
    vec_new = vec_start - outer_rate * (vec_change + outer_momentum * vec_new_momentum)
    return (new_start[None], new_momentum[None], returned, vec_new, vec_new_momentum)


def solution(mesh):
    return jax.shard_map(
        body,
        mesh=mesh,
        in_specs=(
            P("rep", None, "dev", None),
            P(),
            P("dev", None, None, "rep"),
            P("dev", None, None, "rep"),
            P(),
            P("rep", None, None),
            P(),
            P(),
        ),
        out_specs=(
            P("dev", None, None, "rep"),
            P("dev", None, None, "rep"),
            P(None, "dev", None),
            P(),
            P(),
        ),
        check_vma=False,
    )
```

```python
import jax
import jax.numpy as jnp
from jax import lax
from jax.sharding import PartitionSpec as P
from jax.experimental import pallas as pl

EMB_FIRST = 96


outer_rate = 0.7
outer_momentum = 0.9


def rep_sum(x):
    rep_count = lax.axis_size("rep")
    total = x.astype(jnp.bfloat16)
    step = 1
    while step < rep_count:
        other = lax.ppermute(total, "rep", [(i, i ^ step) for i in range(rep_count)])
        total = total.astype(jnp.float32) + other.astype(jnp.float32)
        step *= 2
        if step < rep_count:
            total = total.astype(jnp.bfloat16)
    return total


def _split_kernel(x_ref, a_ref, b_ref):
    w = a_ref.shape[-1]
    a_ref[0] = x_ref[:, :, :w]
    b_ref[0] = x_ref[:, :, w:]


def split_halves(x, width):
    units, rows, full = x.shape
    quarters = full // (2 * width)
    spec = pl.BlockSpec((1, units, rows, width), lambda q: (q, 0, 0, 0))
    return pl.pallas_call(
        _split_kernel,
        grid=(quarters,),
        in_specs=[pl.BlockSpec((units, rows, 2 * width), lambda q: (0, 0, q))],
        out_specs=[spec, spec],
        out_shape=[jax.ShapeDtypeStruct((quarters, units, rows, width), x.dtype)] * 2,
    )(x)


def _join_kernel(a_ref, b_ref, o_ref):
    w = a_ref.shape[-1]
    o_ref[:, :, :w] = a_ref[...]
    o_ref[:, :, w:] = b_ref[...]


def join_halves(a, b, width):
    units, rows, part = a.shape
    quarters = part // width
    spec = pl.BlockSpec((units, rows, width), lambda q: (0, 0, q))
    return pl.pallas_call(
        _join_kernel,
        grid=(quarters,),
        in_specs=[spec, spec],
        out_specs=pl.BlockSpec((units, rows, 2 * width), lambda q: (0, 0, q)),
        out_shape=jax.ShapeDtypeStruct((units, rows, 2 * part), a.dtype),
    )(a, b)


def body(group_weights, owner, start_weights, momentum, basis, vec_groups, vec_start, vec_momentum):
    dev_count = lax.axis_size("dev")
    rep_count = lax.axis_size("rep")
    unit_count = owner.shape[0]
    slot_count = start_weights.shape[1]
    quarter = start_weights.shape[3]
    unit_ids = jnp.arange(unit_count, dtype=jnp.int32)
    same_owner = owner[:, None] == owner[None, :]
    earlier = unit_ids[None, :] < unit_ids[:, None]
    slot_of = jnp.sum((same_owner & earlier).astype(jnp.int32), axis=1)
    target = owner * slot_count + slot_of
    positions = jnp.arange(dev_count * slot_count, dtype=jnp.int32)
    placed = target[:, None] == positions[None, :]
    source_unit = jnp.sum(jnp.where(placed, unit_ids[:, None], 0), axis=0)
    own_rows = group_weights[0]
    width = quarter // 2
    halves = split_halves(own_rows, width)
    arrived_parts = []
    for half in halves:
        summed = lax.psum_scatter(half, "rep", scatter_dimension=0, tiled=True)[0]
        picked = jnp.take(summed, source_unit, axis=0, mode="clip")
        arrived_parts.append(lax.all_to_all(
            picked.reshape(dev_count, slot_count, summed.shape[1], summed.shape[2]),
            "dev",
            split_axis=0,
            concat_axis=2,
            tiled=True,
        ))
    arrived = jnp.concatenate(arrived_parts, axis=3)
    group_mean = arrived[0].astype(jnp.float32) / rep_count
    start_rows = start_weights[0]
    momentum_rows = momentum[0]
    my_slots = lax.axis_index("dev") * slot_count + jnp.arange(slot_count, dtype=jnp.int32)
    own_placed = target[:, None] == my_slots[None, :]
    is_owned = jnp.any(own_placed, axis=0)
    is_embedding = jnp.any(own_placed & (unit_ids >= EMB_FIRST)[:, None], axis=0)
    change = start_rows - group_mean
    first_column = lax.axis_index("rep") * quarter
    basis_part = lax.dynamic_slice_in_dim(basis, first_column, quarter, 1)
    coeff_terms = jnp.einsum("sbq,kq->sbk", change, basis_part, precision=lax.Precision.HIGHEST)
    vec_terms = vec_groups[0]
    coeff_flat = coeff_terms.astype(jnp.bfloat16).reshape(-1)
    joined = rep_sum(jnp.concatenate([coeff_flat, vec_terms.reshape(-1)]))
    coeffs = joined[: coeff_flat.shape[0]].reshape(coeff_terms.shape)
    vec_summed = joined[coeff_flat.shape[0]:].reshape(vec_terms.shape)
    projected = jnp.einsum("sbk,kq->sbq", coeffs, basis_part, precision=lax.Precision.HIGHEST)
    outer_grad = jnp.where(is_embedding[:, None, None], projected, change)
    fresh_momentum = outer_momentum * momentum_rows + outer_grad
    fresh_start = start_rows - outer_rate * (outer_grad + outer_momentum * fresh_momentum)
    owned_mask = is_owned[:, None, None]
    new_momentum = jnp.where(owned_mask, fresh_momentum, momentum_rows)
    new_start = jnp.where(owned_mask, fresh_start, start_rows)
    rounded = fresh_start.astype(jnp.bfloat16)
    gathered = []
    for c in range(2):
        pieces = lax.all_to_all(rounded[:, :, c * width:(c + 1) * width], "dev", split_axis=1, concat_axis=0, tiled=True)
        picked = jnp.take(pieces, target, axis=0, mode="clip")
        gathered.append(lax.all_gather(picked, "rep", axis=2, tiled=True))
    returned = join_halves(gathered[0], gathered[1], width)
    vec_change = vec_start - vec_summed / rep_count
    vec_new_momentum = outer_momentum * vec_momentum + vec_change
    vec_new = vec_start - outer_rate * (vec_change + outer_momentum * vec_new_momentum)
    return (new_start[None], new_momentum[None], returned, vec_new, vec_new_momentum)


def solution(mesh):
    return jax.shard_map(
        body,
        mesh=mesh,
        in_specs=(
            P("rep", None, "dev", None),
            P(),
            P("dev", None, None, "rep"),
            P("dev", None, None, "rep"),
            P(),
            P("rep", None, None),
            P(),
            P(),
        ),
        out_specs=(
            P("dev", None, None, "rep"),
            P("dev", None, None, "rep"),
            P(None, "dev", None),
            P(),
            P(),
        ),
        check_vma=False,
    )
```

```python
import jax
import jax.numpy as jnp
from jax import lax
from jax.sharding import PartitionSpec as P
from jax.experimental import pallas as pl

EMB_FIRST = 96


outer_rate = 0.7
outer_momentum = 0.9


def rep_sum(x):
    rep_count = lax.axis_size("rep")
    total = x.astype(jnp.bfloat16)
    step = 1
    while step < rep_count:
        other = lax.ppermute(total, "rep", [(i, i ^ step) for i in range(rep_count)])
        total = total.astype(jnp.float32) + other.astype(jnp.float32)
        step *= 2
        if step < rep_count:
            total = total.astype(jnp.bfloat16)
    return total


def _copy_kernel(x_ref, o_ref):
    o_ref[...] = x_ref[...].reshape(o_ref.shape)


def take_half(x, width, half):
    units, rows, full = x.shape
    quarters = full // (2 * width)
    return pl.pallas_call(
        _copy_kernel,
        grid=(quarters,),
        in_specs=[pl.BlockSpec((units, rows, width), lambda q: (0, 0, 2 * q + half))],
        out_specs=pl.BlockSpec((1, units, rows, width), lambda q: (q, 0, 0, 0)),
        out_shape=jax.ShapeDtypeStruct((quarters, units, rows, width), x.dtype),
    )(x)


def _place_kernel(a_ref, base_ref, o_ref):
    del base_ref
    o_ref[...] = a_ref[...]


def place_half(a, width, half, base=None):
    units, rows, part = a.shape
    quarters = part // width
    in_spec = pl.BlockSpec((units, rows, width), lambda q: (0, 0, q))
    out_spec = pl.BlockSpec((units, rows, width), lambda q: (0, 0, 2 * q + half))
    out_shape = jax.ShapeDtypeStruct((units, rows, 2 * part), a.dtype)
    if base is None:
        return pl.pallas_call(
            _copy_kernel, grid=(quarters,), in_specs=[in_spec], out_specs=out_spec, out_shape=out_shape
        )(a)
    return pl.pallas_call(
        _place_kernel,
        grid=(quarters,),
        in_specs=[in_spec, pl.BlockSpec(memory_space=pl.ANY)],
        out_specs=out_spec,
        out_shape=out_shape,
        input_output_aliases={1: 0},
    )(a, base)


def body(group_weights, owner, start_weights, momentum, basis, vec_groups, vec_start, vec_momentum):
    dev_count = lax.axis_size("dev")
    rep_count = lax.axis_size("rep")
    unit_count = owner.shape[0]
    slot_count = start_weights.shape[1]
    quarter = start_weights.shape[3]
    unit_ids = jnp.arange(unit_count, dtype=jnp.int32)
    same_owner = owner[:, None] == owner[None, :]
    earlier = unit_ids[None, :] < unit_ids[:, None]
    slot_of = jnp.sum((same_owner & earlier).astype(jnp.int32), axis=1)
    target = owner * slot_count + slot_of
    positions = jnp.arange(dev_count * slot_count, dtype=jnp.int32)
    placed = target[:, None] == positions[None, :]
    source_unit = jnp.sum(jnp.where(placed, unit_ids[:, None], 0), axis=0)
    own_rows = group_weights[0]
    width = quarter // 2
    arrived_parts = []
    for c in range(2):
        half = take_half(own_rows, width, c)
        summed = lax.psum_scatter(half, "rep", scatter_dimension=0, tiled=True)[0]
        picked = jnp.take(summed, source_unit, axis=0, mode="clip")
        arrived_parts.append(lax.all_to_all(
            picked.reshape(dev_count, slot_count, summed.shape[1], summed.shape[2]),
            "dev",
            split_axis=0,
            concat_axis=2,
            tiled=True,
        ))
    arrived = jnp.concatenate(arrived_parts, axis=3)
    group_mean = arrived[0].astype(jnp.float32) / rep_count
    start_rows = start_weights[0]
    momentum_rows = momentum[0]
    my_slots = lax.axis_index("dev") * slot_count + jnp.arange(slot_count, dtype=jnp.int32)
    own_placed = target[:, None] == my_slots[None, :]
    is_owned = jnp.any(own_placed, axis=0)
    is_embedding = jnp.any(own_placed & (unit_ids >= EMB_FIRST)[:, None], axis=0)
    change = start_rows - group_mean
    first_column = lax.axis_index("rep") * quarter
    basis_part = lax.dynamic_slice_in_dim(basis, first_column, quarter, 1)
    coeff_terms = jnp.einsum("sbq,kq->sbk", change, basis_part, precision=lax.Precision.HIGH)
    vec_terms = vec_groups[0]
    coeff_flat = coeff_terms.astype(jnp.bfloat16).reshape(-1)
    joined = rep_sum(jnp.concatenate([coeff_flat, vec_terms.reshape(-1)]))
    coeffs = joined[: coeff_flat.shape[0]].reshape(coeff_terms.shape)
    vec_summed = joined[coeff_flat.shape[0]:].reshape(vec_terms.shape)
    projected = jnp.einsum("sbk,kq->sbq", coeffs, basis_part, precision=lax.Precision.HIGH)
    outer_grad = jnp.where(is_embedding[:, None, None], projected, change)
    fresh_momentum = outer_momentum * momentum_rows + outer_grad
    fresh_start = start_rows - outer_rate * (outer_grad + outer_momentum * fresh_momentum)
    owned_mask = is_owned[:, None, None]
    new_momentum = jnp.where(owned_mask, fresh_momentum, momentum_rows)
    new_start = jnp.where(owned_mask, fresh_start, start_rows)
    rounded = fresh_start.astype(jnp.bfloat16)
    returned = None
    for c in range(2):
        pieces = lax.all_to_all(rounded[:, :, c * width:(c + 1) * width], "dev", split_axis=1, concat_axis=0, tiled=True)
        picked = jnp.take(pieces, target, axis=0, mode="clip")
        gathered = lax.all_gather(picked, "rep", axis=2, tiled=True)
        returned = place_half(gathered, width, c, returned)
    vec_change = vec_start - vec_summed / rep_count
    vec_new_momentum = outer_momentum * vec_momentum + vec_change
    vec_new = vec_start - outer_rate * (vec_change + outer_momentum * vec_new_momentum)
    return (new_start[None], new_momentum[None], returned, vec_new, vec_new_momentum)


def solution(mesh):
    return jax.shard_map(
        body,
        mesh=mesh,
        in_specs=(
            P("rep", None, "dev", None),
            P(),
            P("dev", None, None, "rep"),
            P("dev", None, None, "rep"),
            P(),
            P("rep", None, None),
            P(),
            P(),
        ),
        out_specs=(
            P("dev", None, None, "rep"),
            P("dev", None, None, "rep"),
            P(None, "dev", None),
            P(),
            P(),
        ),
        check_vma=False,
    )
```

```python
import jax
import jax.numpy as jnp
from jax import lax
from jax.sharding import PartitionSpec as P
from jax.experimental import pallas as pl

EMB_FIRST = 96


outer_rate = 0.7
outer_momentum = 0.9


def rep_sum(x):
    rep_count = lax.axis_size("rep")
    total = x.astype(jnp.bfloat16)
    step = 1
    while step < rep_count:
        other = lax.ppermute(total, "rep", [(i, i ^ step) for i in range(rep_count)])
        total = total.astype(jnp.float32) + other.astype(jnp.float32)
        step *= 2
        if step < rep_count:
            total = total.astype(jnp.bfloat16)
    return total


def _copy_kernel(x_ref, o_ref):
    o_ref[...] = x_ref[...].reshape(o_ref.shape)


def take_half(x, width, half):
    units, rows, full = x.shape
    quarters = full // (2 * width)
    return pl.pallas_call(
        _copy_kernel,
        grid=(quarters,),
        in_specs=[pl.BlockSpec((units, rows, width), lambda q: (0, 0, 2 * q + half))],
        out_specs=pl.BlockSpec((1, units, rows, width), lambda q: (q, 0, 0, 0)),
        out_shape=jax.ShapeDtypeStruct((quarters, units, rows, width), x.dtype),
    )(x)


def _place_kernel(a_ref, base_ref, o_ref):
    del base_ref
    o_ref[...] = a_ref[...]


def place_half(a, width, half, base=None):
    units, rows, part = a.shape
    quarters = part // width
    in_spec = pl.BlockSpec((units, rows, width), lambda q: (0, 0, q))
    out_spec = pl.BlockSpec((units, rows, width), lambda q: (0, 0, 2 * q + half))
    out_shape = jax.ShapeDtypeStruct((units, rows, 2 * part), a.dtype)
    if base is None:
        return pl.pallas_call(
            _copy_kernel, grid=(quarters,), in_specs=[in_spec], out_specs=out_spec, out_shape=out_shape
        )(a)
    return pl.pallas_call(
        _place_kernel,
        grid=(quarters,),
        in_specs=[in_spec, pl.BlockSpec(memory_space=pl.ANY)],
        out_specs=out_spec,
        out_shape=out_shape,
        input_output_aliases={1: 0},
    )(a, base)


def body(group_weights, owner, start_weights, momentum, basis, vec_groups, vec_start, vec_momentum):
    dev_count = lax.axis_size("dev")
    rep_count = lax.axis_size("rep")
    unit_count = owner.shape[0]
    slot_count = start_weights.shape[1]
    quarter = start_weights.shape[3]
    unit_ids = jnp.arange(unit_count, dtype=jnp.int32)
    same_owner = owner[:, None] == owner[None, :]
    earlier = unit_ids[None, :] < unit_ids[:, None]
    slot_of = jnp.sum((same_owner & earlier).astype(jnp.int32), axis=1)
    target = owner * slot_count + slot_of
    positions = jnp.arange(dev_count * slot_count, dtype=jnp.int32)
    placed = target[:, None] == positions[None, :]
    source_unit = jnp.sum(jnp.where(placed, unit_ids[:, None], 0), axis=0)
    own_rows = group_weights[0]
    width = quarter // 2
    start_rows = start_weights[0]
    momentum_rows = momentum[0]
    my_slots = lax.axis_index("dev") * slot_count + jnp.arange(slot_count, dtype=jnp.int32)
    own_placed = target[:, None] == my_slots[None, :]
    is_owned = jnp.any(own_placed, axis=0)
    is_embedding = jnp.any(own_placed & (unit_ids >= EMB_FIRST)[:, None], axis=0)
    first_column = lax.axis_index("rep") * quarter
    basis_part = lax.dynamic_slice_in_dim(basis, first_column, quarter, 1)
    halves = [slice(c * width, (c + 1) * width) for c in range(2)]
    changes = []
    coeff_terms = None
    for c in range(2):
        half = take_half(own_rows, width, c)
        summed = lax.psum_scatter(half, "rep", scatter_dimension=0, tiled=True)[0]
        picked = jnp.take(summed, source_unit, axis=0, mode="clip")
        arrived = lax.all_to_all(
            picked.reshape(dev_count, slot_count, summed.shape[1], summed.shape[2]),
            "dev",
            split_axis=0,
            concat_axis=2,
            tiled=True,
        )
        change = start_rows[:, :, halves[c]] - arrived[0].astype(jnp.float32) / rep_count
        changes.append(change)
        term = jnp.einsum("sbq,kq->skb", change, basis_part[:, halves[c]], precision=lax.Precision.HIGH)
        coeff_terms = term if coeff_terms is None else coeff_terms + term
    rank = coeff_terms.shape[1]
    rows_all = coeff_terms.shape[2]
    vec_terms = vec_groups[0]
    vec_rows = vec_terms.shape[0]
    vec_padded = jnp.pad(vec_terms, ((0, (-vec_rows) % 16), (0, 0)))
    coeff_block = coeff_terms.astype(jnp.bfloat16).reshape(slot_count * rank, rows_all)
    vec_block = vec_padded.reshape(-1, rows_all)
    joined = rep_sum(jnp.concatenate([coeff_block, vec_block], axis=0))
    coeffs = joined[: slot_count * rank].reshape(slot_count, rank, rows_all)
    vec_summed = joined[slot_count * rank:].reshape(vec_padded.shape)[:vec_rows]
    owned_mask = is_owned[:, None, None]
    emb_mask = is_embedding[:, None, None]

    def fresh(c):
        projected = jnp.einsum("skb,kq->sbq", coeffs, basis_part[:, halves[c]], precision=lax.Precision.HIGH)
        outer_grad = jnp.where(emb_mask, projected, changes[c])
        fresh_momentum = outer_momentum * momentum_rows[:, :, halves[c]] + outer_grad
        fresh_start = start_rows[:, :, halves[c]] - outer_rate * (outer_grad + outer_momentum * fresh_momentum)
        return fresh_start, fresh_momentum

    returned = None
    new_starts, new_momenta = [], []
    for c in range(2):
        fresh_start, fresh_momentum = fresh(c)
        new_momenta.append(jnp.where(owned_mask, fresh_momentum, momentum_rows[:, :, halves[c]]))
        new_starts.append(jnp.where(owned_mask, fresh_start, start_rows[:, :, halves[c]]))
        rounded = fresh_start.astype(jnp.bfloat16)
        pieces = lax.all_to_all(rounded, "dev", split_axis=1, concat_axis=0, tiled=True)
        picked = jnp.take(pieces, target, axis=0, mode="clip")
        gathered = lax.all_gather(picked, "rep", axis=2, tiled=True)
        returned = place_half(gathered, width, c, returned)
    new_start = jnp.concatenate(new_starts, axis=2)
    new_momentum = jnp.concatenate(new_momenta, axis=2)
    vec_change = vec_start - vec_summed / rep_count
    vec_new_momentum = outer_momentum * vec_momentum + vec_change
    vec_new = vec_start - outer_rate * (vec_change + outer_momentum * vec_new_momentum)
    return (new_start[None], new_momentum[None], returned, vec_new, vec_new_momentum)


def solution(mesh):
    return jax.shard_map(
        body,
        mesh=mesh,
        in_specs=(
            P("rep", None, "dev", None),
            P(),
            P("dev", None, None, "rep"),
            P("dev", None, None, "rep"),
            P(),
            P("rep", None, None),
            P(),
            P(),
        ),
        out_specs=(
            P("dev", None, None, "rep"),
            P("dev", None, None, "rep"),
            P(None, "dev", None),
            P(),
            P(),
        ),
        check_vma=False,
    )
```

```python
import jax
import jax.numpy as jnp
from jax import lax
from jax.sharding import PartitionSpec as P
from jax.experimental import pallas as pl

EMB_FIRST = 96


outer_rate = 0.7
outer_momentum = 0.9


def rep_sum(x):
    rep_count = lax.axis_size("rep")
    total = x.astype(jnp.bfloat16)
    step = 1
    while step < rep_count:
        other = lax.ppermute(total, "rep", [(i, i ^ step) for i in range(rep_count)])
        total = total.astype(jnp.float32) + other.astype(jnp.float32)
        step *= 2
        if step < rep_count:
            total = total.astype(jnp.bfloat16)
    return total


def _copy_kernel(x_ref, o_ref):
    o_ref[...] = x_ref[...].reshape(o_ref.shape)


def take_half(x, width, half):
    units, rows, full = x.shape
    quarters = full // (2 * width)
    return pl.pallas_call(
        _copy_kernel,
        grid=(quarters,),
        in_specs=[pl.BlockSpec((units, rows, width), lambda q: (0, 0, 2 * q + half))],
        out_specs=pl.BlockSpec((1, units, rows, width), lambda q: (q, 0, 0, 0)),
        out_shape=jax.ShapeDtypeStruct((quarters, units, rows, width), x.dtype),
    )(x)


def _place_kernel(a_ref, base_ref, o_ref):
    del base_ref
    o_ref[...] = a_ref[...]


def place_half(a, width, half, base=None):
    units, rows, part = a.shape
    quarters = part // width
    in_spec = pl.BlockSpec((units, rows, width), lambda q: (0, 0, q))
    out_spec = pl.BlockSpec((units, rows, width), lambda q: (0, 0, 2 * q + half))
    out_shape = jax.ShapeDtypeStruct((units, rows, 2 * part), a.dtype)
    if base is None:
        return pl.pallas_call(
            _copy_kernel, grid=(quarters,), in_specs=[in_spec], out_specs=out_spec, out_shape=out_shape
        )(a)
    return pl.pallas_call(
        _place_kernel,
        grid=(quarters,),
        in_specs=[in_spec, pl.BlockSpec(memory_space=pl.ANY)],
        out_specs=out_spec,
        out_shape=out_shape,
        input_output_aliases={1: 0},
    )(a, base)


def body(group_weights, owner, start_weights, momentum, basis, vec_groups, vec_start, vec_momentum):
    dev_count = lax.axis_size("dev")
    rep_count = lax.axis_size("rep")
    unit_count = owner.shape[0]
    slot_count = start_weights.shape[1]
    quarter = start_weights.shape[3]
    unit_ids = jnp.arange(unit_count, dtype=jnp.int32)
    same_owner = owner[:, None] == owner[None, :]
    earlier = unit_ids[None, :] < unit_ids[:, None]
    slot_of = jnp.sum((same_owner & earlier).astype(jnp.int32), axis=1)
    target = owner * slot_count + slot_of
    positions = jnp.arange(dev_count * slot_count, dtype=jnp.int32)
    placed = target[:, None] == positions[None, :]
    source_unit = jnp.sum(jnp.where(placed, unit_ids[:, None], 0), axis=0)
    own_rows = group_weights[0]
    width = quarter // 2
    start_rows = start_weights[0]
    momentum_rows = momentum[0]
    my_slots = lax.axis_index("dev") * slot_count + jnp.arange(slot_count, dtype=jnp.int32)
    own_placed = target[:, None] == my_slots[None, :]
    is_owned = jnp.any(own_placed, axis=0)
    is_embedding = jnp.any(own_placed & (unit_ids >= EMB_FIRST)[:, None], axis=0)
    first_column = lax.axis_index("rep") * quarter
    basis_part = lax.dynamic_slice_in_dim(basis, first_column, quarter, 1)
    halves = [slice(c * width, (c + 1) * width) for c in range(2)]
    changes = []
    coeff_terms = None
    for c in range(2):
        half = take_half(own_rows, width, c)
        summed = lax.psum_scatter(half, "rep", scatter_dimension=0, tiled=True)[0]
        picked = jnp.take(summed, source_unit, axis=0, mode="clip")
        arrived = lax.all_to_all(
            picked.reshape(dev_count, slot_count, summed.shape[1], summed.shape[2]),
            "dev",
            split_axis=0,
            concat_axis=2,
            tiled=True,
        )
        change = start_rows[:, :, halves[c]] - arrived[0].astype(jnp.float32) / rep_count
        changes.append(change)
        term = jnp.einsum("sbq,kq->skb", change, basis_part[:, halves[c]], precision=lax.Precision.HIGH)
        coeff_terms = term if coeff_terms is None else coeff_terms + term
    rank = coeff_terms.shape[1]
    rows_all = coeff_terms.shape[2]
    vec_terms = vec_groups[0]
    vec_rows = vec_terms.shape[0]
    vec_padded = jnp.pad(vec_terms, ((0, (-vec_rows) % 16), (0, 0)))
    coeff_block = coeff_terms.astype(jnp.bfloat16).reshape(slot_count * rank, rows_all)
    vec_block = vec_padded.reshape(-1, rows_all)
    joined = rep_sum(jnp.concatenate([coeff_block, vec_block], axis=0))
    coeffs = joined[: slot_count * rank].reshape(slot_count, rank, rows_all)
    vec_summed = joined[slot_count * rank:].reshape(vec_padded.shape)[:vec_rows]
    owned_mask = is_owned[:, None, None]
    emb_mask = is_embedding[:, None, None]

    def fresh(start_part, momentum_part, change, basis_cols):
        projected = jnp.einsum("skb,kq->sbq", coeffs, basis_cols, precision=lax.Precision.HIGH)
        outer_grad = jnp.where(emb_mask, projected, change)
        fresh_momentum = outer_momentum * momentum_part + outer_grad
        fresh_start = start_part - outer_rate * (outer_grad + outer_momentum * fresh_momentum)
        return fresh_start, fresh_momentum

    returned = None
    for c in range(2):
        fresh_start, _ = fresh(start_rows[:, :, halves[c]], momentum_rows[:, :, halves[c]], changes[c], basis_part[:, halves[c]])
        rounded = fresh_start.astype(jnp.bfloat16)
        pieces = lax.all_to_all(rounded, "dev", split_axis=1, concat_axis=0, tiled=True)
        picked = jnp.take(pieces, target, axis=0, mode="clip")
        gathered = lax.all_gather(picked, "rep", axis=2, tiled=True)
        if c == 0:
            late_inputs = lax.optimization_barrier((start_rows, momentum_rows, changes[0], changes[1], gathered))
            gathered = late_inputs[4]
        returned = place_half(gathered, width, c, returned)
    late_start, late_momentum, late_change0, late_change1, _ = late_inputs
    fresh_start, fresh_momentum = fresh(late_start, late_momentum, jnp.concatenate([late_change0, late_change1], axis=2), basis_part)
    new_momentum = jnp.where(owned_mask, fresh_momentum, late_momentum)
    new_start = jnp.where(owned_mask, fresh_start, late_start)
    vec_change = vec_start - vec_summed / rep_count
    vec_new_momentum = outer_momentum * vec_momentum + vec_change
    vec_new = vec_start - outer_rate * (vec_change + outer_momentum * vec_new_momentum)
    return (new_start[None], new_momentum[None], returned, vec_new, vec_new_momentum)


def solution(mesh):
    return jax.shard_map(
        body,
        mesh=mesh,
        in_specs=(
            P("rep", None, "dev", None),
            P(),
            P("dev", None, None, "rep"),
            P("dev", None, None, "rep"),
            P(),
            P("rep", None, None),
            P(),
            P(),
        ),
        out_specs=(
            P("dev", None, None, "rep"),
            P("dev", None, None, "rep"),
            P(None, "dev", None),
            P(),
            P(),
        ),
        check_vma=False,
    )
```

```python
import jax
import jax.numpy as jnp
from jax import lax
from jax.sharding import PartitionSpec as P
from jax.experimental import pallas as pl

EMB_FIRST = 96


outer_rate = 0.7
outer_momentum = 0.9


def rep_sum(x):
    rep_count = lax.axis_size("rep")
    total = x.astype(jnp.bfloat16)
    step = 1
    while step < rep_count:
        other = lax.ppermute(total, "rep", [(i, i ^ step) for i in range(rep_count)])
        total = total.astype(jnp.float32) + other.astype(jnp.float32)
        step *= 2
        if step < rep_count:
            total = total.astype(jnp.bfloat16)
    return total


def _copy_kernel(x_ref, o_ref):
    o_ref[...] = x_ref[...].reshape(o_ref.shape)


def take_half(x, width, half):
    units, rows, full = x.shape
    quarters = full // (2 * width)
    return pl.pallas_call(
        _copy_kernel,
        grid=(quarters,),
        in_specs=[pl.BlockSpec((units, rows, width), lambda q: (0, 0, 2 * q + half))],
        out_specs=pl.BlockSpec((1, units, rows, width), lambda q: (q, 0, 0, 0)),
        out_shape=jax.ShapeDtypeStruct((quarters, units, rows, width), x.dtype),
    )(x)


def _place_kernel(a_ref, base_ref, o_ref):
    del base_ref
    o_ref[...] = a_ref[...]


def place_half(a, width, half, base=None):
    units, rows, part = a.shape
    quarters = part // width
    in_spec = pl.BlockSpec((units, rows, width), lambda q: (0, 0, q))
    out_spec = pl.BlockSpec((units, rows, width), lambda q: (0, 0, 2 * q + half))
    out_shape = jax.ShapeDtypeStruct((units, rows, 2 * part), a.dtype)
    if base is None:
        return pl.pallas_call(
            _copy_kernel, grid=(quarters,), in_specs=[in_spec], out_specs=out_spec, out_shape=out_shape
        )(a)
    return pl.pallas_call(
        _place_kernel,
        grid=(quarters,),
        in_specs=[in_spec, pl.BlockSpec(memory_space=pl.ANY)],
        out_specs=out_spec,
        out_shape=out_shape,
        input_output_aliases={1: 0},
    )(a, base)


def body(group_weights, owner, start_weights, momentum, basis, vec_groups, vec_start, vec_momentum):
    dev_count = lax.axis_size("dev")
    rep_count = lax.axis_size("rep")
    unit_count = owner.shape[0]
    slot_count = start_weights.shape[1]
    quarter = start_weights.shape[3]
    unit_ids = jnp.arange(unit_count, dtype=jnp.int32)
    same_owner = owner[:, None] == owner[None, :]
    earlier = unit_ids[None, :] < unit_ids[:, None]
    slot_of = jnp.sum((same_owner & earlier).astype(jnp.int32), axis=1)
    target = owner * slot_count + slot_of
    positions = jnp.arange(dev_count * slot_count, dtype=jnp.int32)
    placed = target[:, None] == positions[None, :]
    source_unit = jnp.sum(jnp.where(placed, unit_ids[:, None], 0), axis=0)
    own_rows = group_weights[0]
    width = quarter // 2
    start_rows = start_weights[0]
    momentum_rows = momentum[0]
    my_slots = lax.axis_index("dev") * slot_count + jnp.arange(slot_count, dtype=jnp.int32)
    own_placed = target[:, None] == my_slots[None, :]
    is_owned = jnp.any(own_placed, axis=0)
    is_embedding = jnp.any(own_placed & (unit_ids >= EMB_FIRST)[:, None], axis=0)
    first_column = lax.axis_index("rep") * quarter
    basis_part = lax.dynamic_slice_in_dim(basis, first_column, quarter, 1)
    halves = [slice(c * width, (c + 1) * width) for c in range(2)]
    changes = []
    coeff_terms = None
    for c in range(2):
        half = take_half(own_rows, width, c)
        summed = lax.psum_scatter(half, "rep", scatter_dimension=0, tiled=True)[0]
        picked = jnp.take(summed, source_unit, axis=0, mode="clip")
        arrived = lax.all_to_all(
            picked.reshape(dev_count, slot_count, summed.shape[1], summed.shape[2]),
            "dev",
            split_axis=0,
            concat_axis=2,
            tiled=True,
        )
        change = start_rows[:, :, halves[c]] - arrived[0].astype(jnp.float32) / rep_count
        changes.append(change)
        term = jnp.einsum("sbq,kq->skb", change, basis_part[:, halves[c]], precision=lax.Precision.HIGH)
        coeff_terms = term if coeff_terms is None else coeff_terms + term
    rank = coeff_terms.shape[1]
    rows_all = coeff_terms.shape[2]
    vec_terms = vec_groups[0]
    vec_rows = vec_terms.shape[0]
    vec_padded = jnp.pad(vec_terms, ((0, (-vec_rows) % 16), (0, 0)))
    coeff_block = coeff_terms.astype(jnp.bfloat16).reshape(slot_count * rank, rows_all)
    vec_block = vec_padded.reshape(-1, rows_all)
    joined = rep_sum(jnp.concatenate([coeff_block, vec_block], axis=0))
    coeffs = joined[: slot_count * rank].reshape(slot_count, rank, rows_all)
    vec_summed = joined[slot_count * rank:].reshape(vec_padded.shape)[:vec_rows]
    owned_mask = is_owned[:, None, None]
    emb_mask = is_embedding[:, None, None]

    def fresh(start_part, momentum_part, change, basis_cols):
        projected = jnp.einsum("skb,kq->sbq", coeffs, basis_cols, precision=lax.Precision.HIGH)
        outer_grad = jnp.where(emb_mask, projected, change)
        fresh_momentum = outer_momentum * momentum_part + outer_grad
        fresh_start = start_part - outer_rate * (outer_grad + outer_momentum * fresh_momentum)
        return fresh_start, fresh_momentum

    returned = None
    all_changes = jnp.concatenate(changes, axis=2)
    rounded_all = fresh(start_rows, momentum_rows, all_changes, basis_part)[0].astype(jnp.bfloat16)
    for c in range(2):
        rounded = rounded_all[:, :, halves[c]]
        pieces = lax.all_to_all(rounded, "dev", split_axis=1, concat_axis=0, tiled=True)
        picked = jnp.take(pieces, target, axis=0, mode="clip")
        gathered = lax.all_gather(picked, "rep", axis=2, tiled=True)
        if c == 0:
            late_inputs = lax.optimization_barrier((start_rows, momentum_rows, changes[0], changes[1], gathered))
            gathered = late_inputs[4]
        returned = place_half(gathered, width, c, returned)
    late_start, late_momentum, late_change0, late_change1, _ = late_inputs
    fresh_start, fresh_momentum = fresh(late_start, late_momentum, jnp.concatenate([late_change0, late_change1], axis=2), basis_part)
    new_momentum = jnp.where(owned_mask, fresh_momentum, late_momentum)
    new_start = jnp.where(owned_mask, fresh_start, late_start)
    vec_change = vec_start - vec_summed / rep_count
    vec_new_momentum = outer_momentum * vec_momentum + vec_change
    vec_new = vec_start - outer_rate * (vec_change + outer_momentum * vec_new_momentum)
    return (new_start[None], new_momentum[None], returned, vec_new, vec_new_momentum)


def solution(mesh):
    return jax.shard_map(
        body,
        mesh=mesh,
        in_specs=(
            P("rep", None, "dev", None),
            P(),
            P("dev", None, None, "rep"),
            P("dev", None, None, "rep"),
            P(),
            P("rep", None, None),
            P(),
            P(),
        ),
        out_specs=(
            P("dev", None, None, "rep"),
            P("dev", None, None, "rep"),
            P(None, "dev", None),
            P(),
            P(),
        ),
        check_vma=False,
    )
```

```python
import jax
import jax.numpy as jnp
from jax import lax
from jax.sharding import PartitionSpec as P
from jax.experimental import pallas as pl

EMB_FIRST = 96


outer_rate = 0.7
outer_momentum = 0.9


def rep_sum(x):
    rep_count = lax.axis_size("rep")
    if rep_count != 4:
        total = x.astype(jnp.bfloat16)
        step = 1
        while step < rep_count:
            other = lax.ppermute(total, "rep", [(i, i ^ step) for i in range(rep_count)])
            total = total.astype(jnp.float32) + other.astype(jnp.float32)
            step *= 2
            if step < rep_count:
                total = total.astype(jnp.bfloat16)
        return total
    core = lax.axis_index("rep") % 2
    mine = x.astype(jnp.bfloat16)
    other = lax.ppermute(mine, "rep", [(i, i ^ 1) for i in range(4)])
    pair = (mine.astype(jnp.float32) + other.astype(jnp.float32)).astype(jnp.bfloat16)
    pair = pair.reshape((2, x.shape[0] // 2) + x.shape[1:])
    part = lax.dynamic_index_in_dim(pair, core, 0, keepdims=False)
    across = lax.ppermute(part, "rep", [(i, i ^ 2) for i in range(4)])
    done = part.astype(jnp.float32) + across.astype(jnp.float32)
    rest = lax.ppermute(done, "rep", [(i, i ^ 1) for i in range(4)])
    first = jnp.where(core == 0, done, rest)
    second = jnp.where(core == 0, rest, done)
    return jnp.concatenate([first, second], axis=0)


def _copy_kernel(x_ref, o_ref):
    o_ref[...] = x_ref[...].reshape(o_ref.shape)


def take_half(x, width, half):
    units, rows, full = x.shape
    quarters = full // (2 * width)
    return pl.pallas_call(
        _copy_kernel,
        grid=(quarters,),
        in_specs=[pl.BlockSpec((units, rows, width), lambda q: (0, 0, 2 * q + half))],
        out_specs=pl.BlockSpec((1, units, rows, width), lambda q: (q, 0, 0, 0)),
        out_shape=jax.ShapeDtypeStruct((quarters, units, rows, width), x.dtype),
    )(x)


def _place_kernel(a_ref, base_ref, o_ref):
    del base_ref
    o_ref[...] = a_ref[...]


def place_half(a, width, half, base=None):
    units, rows, part = a.shape
    quarters = part // width
    in_spec = pl.BlockSpec((units, rows, width), lambda q: (0, 0, q))
    out_spec = pl.BlockSpec((units, rows, width), lambda q: (0, 0, 2 * q + half))
    out_shape = jax.ShapeDtypeStruct((units, rows, 2 * part), a.dtype)
    if base is None:
        return pl.pallas_call(
            _copy_kernel, grid=(quarters,), in_specs=[in_spec], out_specs=out_spec, out_shape=out_shape
        )(a)
    return pl.pallas_call(
        _place_kernel,
        grid=(quarters,),
        in_specs=[in_spec, pl.BlockSpec(memory_space=pl.ANY)],
        out_specs=out_spec,
        out_shape=out_shape,
        input_output_aliases={1: 0},
    )(a, base)


def body(group_weights, owner, start_weights, momentum, basis, vec_groups, vec_start, vec_momentum):
    dev_count = lax.axis_size("dev")
    rep_count = lax.axis_size("rep")
    unit_count = owner.shape[0]
    slot_count = start_weights.shape[1]
    quarter = start_weights.shape[3]
    unit_ids = jnp.arange(unit_count, dtype=jnp.int32)
    same_owner = owner[:, None] == owner[None, :]
    earlier = unit_ids[None, :] < unit_ids[:, None]
    slot_of = jnp.sum((same_owner & earlier).astype(jnp.int32), axis=1)
    target = owner * slot_count + slot_of
    positions = jnp.arange(dev_count * slot_count, dtype=jnp.int32)
    placed = target[:, None] == positions[None, :]
    source_unit = jnp.sum(jnp.where(placed, unit_ids[:, None], 0), axis=0)
    own_rows = group_weights[0]
    width = quarter // 2
    start_rows = start_weights[0]
    momentum_rows = momentum[0]
    my_slots = lax.axis_index("dev") * slot_count + jnp.arange(slot_count, dtype=jnp.int32)
    own_placed = target[:, None] == my_slots[None, :]
    is_owned = jnp.any(own_placed, axis=0)
    is_embedding = jnp.any(own_placed & (unit_ids >= EMB_FIRST)[:, None], axis=0)
    first_column = lax.axis_index("rep") * quarter
    basis_part = lax.dynamic_slice_in_dim(basis, first_column, quarter, 1)
    halves = [slice(c * width, (c + 1) * width) for c in range(2)]
    held = start_rows - (outer_rate * outer_momentum * outer_momentum) * momentum_rows
    changes = []
    coeff_terms = None
    for c in range(2):
        half = take_half(own_rows, width, c)
        summed = lax.psum_scatter(half, "rep", scatter_dimension=0, tiled=True)[0]
        picked = jnp.take(summed, source_unit, axis=0, mode="clip")
        arrived = lax.all_to_all(
            picked.reshape(dev_count, slot_count, summed.shape[1], summed.shape[2]),
            "dev",
            split_axis=0,
            concat_axis=2,
            tiled=True,
        )
        change = start_rows[:, :, halves[c]] - arrived[0].astype(jnp.float32) / rep_count
        changes.append(change)
        term = jnp.einsum("sbq,kq->skb", change, basis_part[:, halves[c]], precision=lax.Precision.HIGH)
        coeff_terms = term if coeff_terms is None else coeff_terms + term
    rank = coeff_terms.shape[1]
    rows_all = coeff_terms.shape[2]
    vec_terms = vec_groups[0]
    vec_rows = vec_terms.shape[0]
    vec_padded = jnp.pad(vec_terms, ((0, (-vec_rows) % 16), (0, 0)))
    coeff_block = coeff_terms.astype(jnp.bfloat16).reshape(slot_count * rank, rows_all)
    vec_block = vec_padded.reshape(-1, rows_all)
    joined = rep_sum(jnp.concatenate([coeff_block, vec_block], axis=0))
    coeffs = joined[: slot_count * rank].reshape(slot_count, rank, rows_all)
    vec_summed = joined[slot_count * rank:].reshape(vec_padded.shape)[:vec_rows]
    owned_mask = is_owned[:, None, None]
    emb_mask = is_embedding[:, None, None]

    def fresh(start_part, momentum_part, change, basis_cols):
        projected = jnp.einsum("skb,kq->sbq", coeffs, basis_cols, precision=lax.Precision.HIGH)
        outer_grad = jnp.where(emb_mask, projected, change)
        fresh_momentum = outer_momentum * momentum_part + outer_grad
        fresh_start = start_part - outer_rate * (outer_grad + outer_momentum * fresh_momentum)
        return fresh_start, fresh_momentum

    returned = None
    all_changes = jnp.concatenate(changes, axis=2)
    projected_all = jnp.einsum("skb,kq->sbq", coeffs, basis_part, precision=lax.Precision.HIGH)
    grad_all = jnp.where(emb_mask, projected_all, all_changes)
    rounded_all = (held - (outer_rate * (1.0 + outer_momentum)) * grad_all).astype(jnp.bfloat16)
    for c in range(2):
        rounded = rounded_all[:, :, halves[c]]
        pieces = lax.all_to_all(rounded, "dev", split_axis=1, concat_axis=0, tiled=True)
        picked = jnp.take(pieces, target, axis=0, mode="clip")
        gathered = lax.all_gather(picked, "rep", axis=2, tiled=True)
        if c == 0:
            late_inputs = lax.optimization_barrier((start_rows, momentum_rows, changes[0], changes[1], gathered))
            gathered = late_inputs[4]
        returned = place_half(gathered, width, c, returned)
    late_start, late_momentum, late_change0, late_change1, _ = late_inputs
    fresh_start, fresh_momentum = fresh(late_start, late_momentum, jnp.concatenate([late_change0, late_change1], axis=2), basis_part)
    new_momentum = jnp.where(owned_mask, fresh_momentum, late_momentum)
    new_start = jnp.where(owned_mask, fresh_start, late_start)
    vec_change = vec_start - vec_summed / rep_count
    vec_new_momentum = outer_momentum * vec_momentum + vec_change
    vec_new = vec_start - outer_rate * (vec_change + outer_momentum * vec_new_momentum)
    return (new_start[None], new_momentum[None], returned, vec_new, vec_new_momentum)


def solution(mesh):
    return jax.shard_map(
        body,
        mesh=mesh,
        in_specs=(
            P("rep", None, "dev", None),
            P(),
            P("dev", None, None, "rep"),
            P("dev", None, None, "rep"),
            P(),
            P("rep", None, None),
            P(),
            P(),
        ),
        out_specs=(
            P("dev", None, None, "rep"),
            P("dev", None, None, "rep"),
            P(None, "dev", None),
            P(),
            P(),
        ),
        check_vma=False,
    )
```

```python
import jax
import jax.numpy as jnp
from jax import lax
from jax.sharding import PartitionSpec as P
from jax.experimental import pallas as pl

EMB_FIRST = 96


outer_rate = 0.7
outer_momentum = 0.9


def rep_sum(x):
    rep_count = lax.axis_size("rep")
    if rep_count != 4:
        total = x.astype(jnp.bfloat16)
        step = 1
        while step < rep_count:
            other = lax.ppermute(total, "rep", [(i, i ^ step) for i in range(rep_count)])
            total = total.astype(jnp.float32) + other.astype(jnp.float32)
            step *= 2
            if step < rep_count:
                total = total.astype(jnp.bfloat16)
        return total
    core = lax.axis_index("rep") % 2
    mine = x.astype(jnp.bfloat16)
    other = lax.ppermute(mine, "rep", [(i, i ^ 1) for i in range(4)])
    pair = (mine.astype(jnp.float32) + other.astype(jnp.float32)).astype(jnp.bfloat16)
    pair = pair.reshape((2, x.shape[0] // 2) + x.shape[1:])
    part = lax.dynamic_index_in_dim(pair, core, 0, keepdims=False)
    across = lax.ppermute(part, "rep", [(i, i ^ 2) for i in range(4)])
    done = part.astype(jnp.float32) + across.astype(jnp.float32)
    rest = lax.ppermute(done, "rep", [(i, i ^ 1) for i in range(4)])
    first = jnp.where(core == 0, done, rest)
    second = jnp.where(core == 0, rest, done)
    return jnp.concatenate([first, second], axis=0)


def _copy_kernel(x_ref, o_ref):
    o_ref[...] = x_ref[...].reshape(o_ref.shape)


def take_half(x, width, half):
    units, rows, full = x.shape
    quarters = full // (2 * width)
    return pl.pallas_call(
        _copy_kernel,
        grid=(quarters,),
        in_specs=[pl.BlockSpec((units, rows, width), lambda q: (0, 0, 2 * q + half))],
        out_specs=pl.BlockSpec((1, units, rows, width), lambda q: (q, 0, 0, 0)),
        out_shape=jax.ShapeDtypeStruct((quarters, units, rows, width), x.dtype),
    )(x)


def _place_kernel(a_ref, base_ref, o_ref):
    del base_ref
    o_ref[...] = a_ref[...]


def place_half(a, width, half, base=None):
    units, rows, part = a.shape
    quarters = part // width
    in_spec = pl.BlockSpec((units, rows, width), lambda q: (0, 0, q))
    out_spec = pl.BlockSpec((units, rows, width), lambda q: (0, 0, 2 * q + half))
    out_shape = jax.ShapeDtypeStruct((units, rows, 2 * part), a.dtype)
    if base is None:
        return pl.pallas_call(
            _copy_kernel, grid=(quarters,), in_specs=[in_spec], out_specs=out_spec, out_shape=out_shape
        )(a)
    return pl.pallas_call(
        _place_kernel,
        grid=(quarters,),
        in_specs=[in_spec, pl.BlockSpec(memory_space=pl.ANY)],
        out_specs=out_spec,
        out_shape=out_shape,
        input_output_aliases={1: 0},
    )(a, base)


def body(group_weights, owner, start_weights, momentum, basis, vec_groups, vec_start, vec_momentum):
    dev_count = lax.axis_size("dev")
    rep_count = lax.axis_size("rep")
    unit_count = owner.shape[0]
    slot_count = start_weights.shape[1]
    quarter = start_weights.shape[3]
    unit_ids = jnp.arange(unit_count, dtype=jnp.int32)
    same_owner = owner[:, None] == owner[None, :]
    earlier = unit_ids[None, :] < unit_ids[:, None]
    slot_of = jnp.sum((same_owner & earlier).astype(jnp.int32), axis=1)
    target = owner * slot_count + slot_of
    positions = jnp.arange(dev_count * slot_count, dtype=jnp.int32)
    placed = target[:, None] == positions[None, :]
    source_unit = jnp.sum(jnp.where(placed, unit_ids[:, None], 0), axis=0)
    own_rows = group_weights[0]
    width = quarter // 2
    start_rows = start_weights[0]
    momentum_rows = momentum[0]
    my_slots = lax.axis_index("dev") * slot_count + jnp.arange(slot_count, dtype=jnp.int32)
    own_placed = target[:, None] == my_slots[None, :]
    is_owned = jnp.any(own_placed, axis=0)
    is_embedding = jnp.any(own_placed & (unit_ids >= EMB_FIRST)[:, None], axis=0)
    first_column = lax.axis_index("rep") * quarter
    basis_part = lax.dynamic_slice_in_dim(basis, first_column, quarter, 1)
    halves = [slice(c * width, (c + 1) * width) for c in range(2)]
    held = start_rows - (outer_rate * outer_momentum * outer_momentum) * momentum_rows
    changes = []
    coeff_terms = None
    for c in range(2):
        half = take_half(own_rows, width, c)
        summed = lax.psum_scatter(half, "rep", scatter_dimension=0, tiled=True)[0]
        picked = jnp.take(summed, source_unit, axis=0, mode="clip")
        arrived = lax.all_to_all(
            picked.reshape(dev_count, slot_count, summed.shape[1], summed.shape[2]),
            "dev",
            split_axis=0,
            concat_axis=2,
            tiled=True,
        )
        change = start_rows[:, :, halves[c]] - arrived[0].astype(jnp.float32) / rep_count
        changes.append(change)
        term = jnp.einsum("sbq,kq->skb", change, basis_part[:, halves[c]], precision=lax.Precision.HIGH)
        coeff_terms = term if coeff_terms is None else coeff_terms + term
    rank = coeff_terms.shape[1]
    rows_all = coeff_terms.shape[2]
    vec_terms = vec_groups[0]
    vec_rows = vec_terms.shape[0]
    vec_padded = jnp.pad(vec_terms, ((0, (-vec_rows) % 16), (0, 0)))
    coeff_block = coeff_terms.astype(jnp.bfloat16).reshape(slot_count * rank, rows_all)
    vec_block = vec_padded.reshape(-1, rows_all)
    joined = rep_sum(jnp.concatenate([coeff_block, vec_block], axis=0))
    coeffs = joined[: slot_count * rank].reshape(slot_count, rank, rows_all)
    vec_summed = joined[slot_count * rank:].reshape(vec_padded.shape)[:vec_rows]
    owned_mask = is_owned[:, None, None]
    emb_mask = is_embedding[:, None, None]

    def fresh(start_part, momentum_part, change, basis_cols):
        projected = jnp.einsum("skb,kq->sbq", coeffs, basis_cols, precision=lax.Precision.HIGH)
        outer_grad = jnp.where(emb_mask, projected, change)
        fresh_momentum = outer_momentum * momentum_part + outer_grad
        fresh_start = start_part - outer_rate * (outer_grad + outer_momentum * fresh_momentum)
        return fresh_start, fresh_momentum

    returned = None
    all_changes = jnp.concatenate(changes, axis=2)
    projected_all = jnp.einsum("skb,kq->sbq", coeffs, basis_part, precision=lax.Precision.HIGH)
    grad_all = jnp.where(emb_mask, projected_all, all_changes)
    rounded_all = (held - (outer_rate * (1.0 + outer_momentum)) * grad_all).astype(jnp.bfloat16)
    slots, rows_all, _ = rounded_all.shape
    outgoing_all = rounded_all.reshape(slots, dev_count, rows_all // dev_count, 2, width).transpose(3, 1, 0, 2, 4)
    for c in range(2):
        pieces = lax.all_to_all(outgoing_all[c], "dev", split_axis=0, concat_axis=0, tiled=True)
        pieces = pieces.reshape(dev_count * slots, rows_all // dev_count, width)
        picked = jnp.take(pieces, target, axis=0, mode="clip")
        gathered = lax.all_gather(picked, "rep", axis=2, tiled=True)
        if c == 0:
            late_inputs = lax.optimization_barrier((start_rows, momentum_rows, changes[0], changes[1], gathered))
            gathered = late_inputs[4]
        returned = place_half(gathered, width, c, returned)
    late_start, late_momentum, late_change0, late_change1, _ = late_inputs
    fresh_start, fresh_momentum = fresh(late_start, late_momentum, jnp.concatenate([late_change0, late_change1], axis=2), basis_part)
    new_momentum = jnp.where(owned_mask, fresh_momentum, late_momentum)
    new_start = jnp.where(owned_mask, fresh_start, late_start)
    vec_change = vec_start - vec_summed / rep_count
    vec_new_momentum = outer_momentum * vec_momentum + vec_change
    vec_new = vec_start - outer_rate * (vec_change + outer_momentum * vec_new_momentum)
    return (new_start[None], new_momentum[None], returned, vec_new, vec_new_momentum)


def solution(mesh):
    return jax.shard_map(
        body,
        mesh=mesh,
        in_specs=(
            P("rep", None, "dev", None),
            P(),
            P("dev", None, None, "rep"),
            P("dev", None, None, "rep"),
            P(),
            P("rep", None, None),
            P(),
            P(),
        ),
        out_specs=(
            P("dev", None, None, "rep"),
            P("dev", None, None, "rep"),
            P(None, "dev", None),
            P(),
            P(),
        ),
        check_vma=False,
    )
```

```python
import jax
import jax.numpy as jnp
from jax import lax
from jax.sharding import PartitionSpec as P
from jax.experimental import pallas as pl

EMB_FIRST = 96


outer_rate = 0.7
outer_momentum = 0.9


def rep_sum(x):
    rep_count = lax.axis_size("rep")
    if rep_count != 4:
        total = x.astype(jnp.bfloat16)
        step = 1
        while step < rep_count:
            other = lax.ppermute(total, "rep", [(i, i ^ step) for i in range(rep_count)])
            total = total.astype(jnp.float32) + other.astype(jnp.float32)
            step *= 2
            if step < rep_count:
                total = total.astype(jnp.bfloat16)
        return total
    core = lax.axis_index("rep") % 2
    mine = x.astype(jnp.bfloat16)
    other = lax.ppermute(mine, "rep", [(i, i ^ 1) for i in range(4)])
    pair = (mine.astype(jnp.float32) + other.astype(jnp.float32)).astype(jnp.bfloat16)
    pair = pair.reshape((2, x.shape[0] // 2) + x.shape[1:])
    part = lax.dynamic_index_in_dim(pair, core, 0, keepdims=False)
    across = lax.ppermute(part, "rep", [(i, i ^ 2) for i in range(4)])
    done = part.astype(jnp.float32) + across.astype(jnp.float32)
    rest = lax.ppermute(done, "rep", [(i, i ^ 1) for i in range(4)])
    first = jnp.where(core == 0, done, rest)
    second = jnp.where(core == 0, rest, done)
    return jnp.concatenate([first, second], axis=0)


def _copy_kernel(x_ref, o_ref):
    o_ref[...] = x_ref[...].reshape(o_ref.shape)


def take_half(x, width, half):
    units, rows, full = x.shape
    quarters = full // (2 * width)
    return pl.pallas_call(
        _copy_kernel,
        grid=(quarters,),
        in_specs=[pl.BlockSpec((units, rows, width), lambda q: (0, 0, 2 * q + half))],
        out_specs=pl.BlockSpec((1, units, rows, width), lambda q: (q, 0, 0, 0)),
        out_shape=jax.ShapeDtypeStruct((quarters, units, rows, width), x.dtype),
    )(x)


def _place_kernel(a_ref, base_ref, o_ref):
    del base_ref
    o_ref[...] = a_ref[...]


def place_half(a, width, half, base=None):
    units, rows, part = a.shape
    quarters = part // width
    in_spec = pl.BlockSpec((units, rows, width), lambda q: (0, 0, q))
    out_spec = pl.BlockSpec((units, rows, width), lambda q: (0, 0, 2 * q + half))
    out_shape = jax.ShapeDtypeStruct((units, rows, 2 * part), a.dtype)
    if base is None:
        return pl.pallas_call(
            _copy_kernel, grid=(quarters,), in_specs=[in_spec], out_specs=out_spec, out_shape=out_shape
        )(a)
    return pl.pallas_call(
        _place_kernel,
        grid=(quarters,),
        in_specs=[in_spec, pl.BlockSpec(memory_space=pl.ANY)],
        out_specs=out_spec,
        out_shape=out_shape,
        input_output_aliases={1: 0},
    )(a, base)


def body(group_weights, owner, start_weights, momentum, basis, vec_groups, vec_start, vec_momentum):
    dev_count = lax.axis_size("dev")
    rep_count = lax.axis_size("rep")
    unit_count = owner.shape[0]
    slot_count = start_weights.shape[1]
    quarter = start_weights.shape[3]
    unit_ids = jnp.arange(unit_count, dtype=jnp.int32)
    same_owner = owner[:, None] == owner[None, :]
    earlier = unit_ids[None, :] < unit_ids[:, None]
    slot_of = jnp.sum((same_owner & earlier).astype(jnp.int32), axis=1)
    target = owner * slot_count + slot_of
    positions = jnp.arange(dev_count * slot_count, dtype=jnp.int32)
    placed = target[:, None] == positions[None, :]
    source_unit = jnp.sum(jnp.where(placed, unit_ids[:, None], 0), axis=0)
    own_rows = group_weights[0]
    width = quarter // 2
    start_rows = start_weights[0]
    momentum_rows = momentum[0]
    my_slots = lax.axis_index("dev") * slot_count + jnp.arange(slot_count, dtype=jnp.int32)
    own_placed = target[:, None] == my_slots[None, :]
    is_owned = jnp.any(own_placed, axis=0)
    is_embedding = jnp.any(own_placed & (unit_ids >= EMB_FIRST)[:, None], axis=0)
    first_column = lax.axis_index("rep") * quarter
    basis_part = lax.dynamic_slice_in_dim(basis, first_column, quarter, 1)
    halves = [slice(c * width, (c + 1) * width) for c in range(2)]
    held = start_rows - (outer_rate * outer_momentum * outer_momentum) * momentum_rows
    changes = []
    coeff_terms = None
    for c in range(2):
        half = take_half(own_rows, width, c)
        summed = lax.psum_scatter(half, "rep", scatter_dimension=0, tiled=True)[0]
        picked = jnp.take(summed, source_unit, axis=0, mode="clip")
        arrived = lax.all_to_all(
            picked.reshape(dev_count, slot_count, summed.shape[1], summed.shape[2]),
            "dev",
            split_axis=0,
            concat_axis=2,
            tiled=True,
        )
        change = start_rows[:, :, halves[c]] - arrived[0].astype(jnp.float32) / rep_count
        changes.append(change)
        term = jnp.einsum("sbq,kq->skb", change, basis_part[:, halves[c]], precision=lax.Precision.HIGH)
        coeff_terms = term if coeff_terms is None else coeff_terms + term
    rank = coeff_terms.shape[1]
    rows_all = coeff_terms.shape[2]
    vec_terms = vec_groups[0]
    vec_rows = vec_terms.shape[0]
    vec_padded = jnp.pad(vec_terms, ((0, (-vec_rows) % 16), (0, 0)))
    coeff_block = coeff_terms.astype(jnp.bfloat16).reshape(slot_count * rank, rows_all)
    vec_block = vec_padded.reshape(-1, rows_all)
    joined = rep_sum(jnp.concatenate([coeff_block, vec_block], axis=0))
    coeffs = joined[: slot_count * rank].reshape(slot_count, rank, rows_all)
    vec_summed = joined[slot_count * rank:].reshape(vec_padded.shape)[:vec_rows]
    owned_mask = is_owned[:, None, None]
    emb_mask = is_embedding[:, None, None]

    def fresh(start_part, momentum_part, change, basis_cols):
        projected = jnp.einsum("skb,kq->sbq", coeffs, basis_cols, precision=lax.Precision.HIGH)
        outer_grad = jnp.where(emb_mask, projected, change)
        fresh_momentum = outer_momentum * momentum_part + outer_grad
        fresh_start = start_part - outer_rate * (outer_grad + outer_momentum * fresh_momentum)
        return fresh_start, fresh_momentum

    returned = None
    all_changes = jnp.concatenate(changes, axis=2)
    projected_all = jnp.einsum("skb,kq->sbq", coeffs, basis_part, precision=lax.Precision.HIGH)
    grad_all = jnp.where(emb_mask, projected_all, all_changes)
    rounded_all = (held - (outer_rate * (1.0 + outer_momentum)) * grad_all).astype(jnp.bfloat16)
    for c in range(2):
        rounded = rounded_all[:, :, halves[c]]
        pieces = lax.all_to_all(rounded, "dev", split_axis=1, concat_axis=0, tiled=True)
        picked = jnp.take(pieces, target, axis=0, mode="clip")
        gathered = lax.all_gather(picked, "rep", axis=2, tiled=True)
        if c == 0:
            late_inputs = lax.optimization_barrier((start_rows, momentum_rows, changes[0], changes[1], coeffs, gathered))
            gathered = late_inputs[5]
        returned = place_half(gathered, width, c, returned)
    late_start, late_momentum, late_change0, late_change1, late_coeffs, _ = late_inputs
    coeffs = late_coeffs
    fresh_start, fresh_momentum = fresh(late_start, late_momentum, jnp.concatenate([late_change0, late_change1], axis=2), basis_part)
    new_momentum = jnp.where(owned_mask, fresh_momentum, late_momentum)
    new_start = jnp.where(owned_mask, fresh_start, late_start)
    vec_change = vec_start - vec_summed / rep_count
    vec_new_momentum = outer_momentum * vec_momentum + vec_change
    vec_new = vec_start - outer_rate * (vec_change + outer_momentum * vec_new_momentum)
    return (new_start[None], new_momentum[None], returned, vec_new, vec_new_momentum)


def solution(mesh):
    return jax.shard_map(
        body,
        mesh=mesh,
        in_specs=(
            P("rep", None, "dev", None),
            P(),
            P("dev", None, None, "rep"),
            P("dev", None, None, "rep"),
            P(),
            P("rep", None, None),
            P(),
            P(),
        ),
        out_specs=(
            P("dev", None, None, "rep"),
            P("dev", None, None, "rep"),
            P(None, "dev", None),
            P(),
            P(),
        ),
        check_vma=False,
    )
```

```python
import jax
import jax.numpy as jnp
from jax import lax
from jax.sharding import PartitionSpec as P
from jax.experimental import pallas as pl

EMB_FIRST = 96


outer_rate = 0.7
outer_momentum = 0.9


def rep_sum(x):
    rep_count = lax.axis_size("rep")
    if rep_count != 4:
        total = x.astype(jnp.bfloat16)
        step = 1
        while step < rep_count:
            other = lax.ppermute(total, "rep", [(i, i ^ step) for i in range(rep_count)])
            total = total.astype(jnp.float32) + other.astype(jnp.float32)
            step *= 2
            if step < rep_count:
                total = total.astype(jnp.bfloat16)
        return total
    core = lax.axis_index("rep") % 2
    mine = x.astype(jnp.bfloat16)
    other = lax.ppermute(mine, "rep", [(i, i ^ 1) for i in range(4)])
    pair = (mine.astype(jnp.float32) + other.astype(jnp.float32)).astype(jnp.bfloat16)
    pair = pair.reshape((2, x.shape[0] // 2) + x.shape[1:])
    part = lax.dynamic_index_in_dim(pair, core, 0, keepdims=False)
    across = lax.ppermute(part, "rep", [(i, i ^ 2) for i in range(4)])
    done = part.astype(jnp.float32) + across.astype(jnp.float32)
    rest = lax.ppermute(done, "rep", [(i, i ^ 1) for i in range(4)])
    first = jnp.where(core == 0, done, rest)
    second = jnp.where(core == 0, rest, done)
    return jnp.concatenate([first, second], axis=0)


def _copy_kernel(x_ref, o_ref):
    o_ref[...] = x_ref[...].reshape(o_ref.shape)


def take_half(x, width, half):
    units, rows, full = x.shape
    quarters = full // (2 * width)
    return pl.pallas_call(
        _copy_kernel,
        grid=(quarters,),
        in_specs=[pl.BlockSpec((units, rows, width), lambda q: (0, 0, 2 * q + half))],
        out_specs=pl.BlockSpec((1, units, rows, width), lambda q: (q, 0, 0, 0)),
        out_shape=jax.ShapeDtypeStruct((quarters, units, rows, width), x.dtype),
    )(x)


def _place_kernel(a_ref, base_ref, o_ref):
    del base_ref
    o_ref[...] = a_ref[...]


def place_half(a, width, half, base=None):
    units, rows, part = a.shape
    quarters = part // width
    in_spec = pl.BlockSpec((units, rows, width), lambda q: (0, 0, q))
    out_spec = pl.BlockSpec((units, rows, width), lambda q: (0, 0, 2 * q + half))
    out_shape = jax.ShapeDtypeStruct((units, rows, 2 * part), a.dtype)
    if base is None:
        return pl.pallas_call(
            _copy_kernel, grid=(quarters,), in_specs=[in_spec], out_specs=out_spec, out_shape=out_shape
        )(a)
    return pl.pallas_call(
        _place_kernel,
        grid=(quarters,),
        in_specs=[in_spec, pl.BlockSpec(memory_space=pl.ANY)],
        out_specs=out_spec,
        out_shape=out_shape,
        input_output_aliases={1: 0},
    )(a, base)


def body(group_weights, owner, start_weights, momentum, basis, vec_groups, vec_start, vec_momentum):
    dev_count = lax.axis_size("dev")
    rep_count = lax.axis_size("rep")
    unit_count = owner.shape[0]
    slot_count = start_weights.shape[1]
    quarter = start_weights.shape[3]
    unit_ids = jnp.arange(unit_count, dtype=jnp.int32)
    same_owner = owner[:, None] == owner[None, :]
    earlier = unit_ids[None, :] < unit_ids[:, None]
    slot_of = jnp.sum((same_owner & earlier).astype(jnp.int32), axis=1)
    target = owner * slot_count + slot_of
    positions = jnp.arange(dev_count * slot_count, dtype=jnp.int32)
    placed = target[:, None] == positions[None, :]
    source_unit = jnp.sum(jnp.where(placed, unit_ids[:, None], 0), axis=0)
    own_rows = group_weights[0]
    width = quarter // 2
    start_rows = start_weights[0]
    momentum_rows = momentum[0]
    my_slots = lax.axis_index("dev") * slot_count + jnp.arange(slot_count, dtype=jnp.int32)
    own_placed = target[:, None] == my_slots[None, :]
    is_owned = jnp.any(own_placed, axis=0)
    is_embedding = jnp.any(own_placed & (unit_ids >= EMB_FIRST)[:, None], axis=0)
    first_column = lax.axis_index("rep") * quarter
    basis_part = lax.dynamic_slice_in_dim(basis, first_column, quarter, 1)
    halves = [slice(c * width, (c + 1) * width) for c in range(2)]
    held = start_rows - (outer_rate * outer_momentum * outer_momentum) * momentum_rows
    changes = []
    coeff_terms = None
    for c in range(2):
        half = take_half(own_rows, width, c)
        summed = lax.psum_scatter(half, "rep", scatter_dimension=0, tiled=True)[0]
        picked = jnp.take(summed, source_unit, axis=0, mode="clip")
        arrived = lax.all_to_all(
            picked.reshape(dev_count, slot_count, summed.shape[1], summed.shape[2]),
            "dev",
            split_axis=0,
            concat_axis=2,
            tiled=True,
        )
        change = start_rows[:, :, halves[c]] - arrived[0].astype(jnp.float32) / rep_count
        changes.append(change)
        term = jnp.einsum("sbq,kq->skb", change, basis_part[:, halves[c]], precision=lax.Precision.HIGH)
        coeff_terms = term if coeff_terms is None else coeff_terms + term
    rank = coeff_terms.shape[1]
    rows_all = coeff_terms.shape[2]
    vec_terms = vec_groups[0]
    vec_rows = vec_terms.shape[0]
    vec_padded = jnp.pad(vec_terms, ((0, (-vec_rows) % 16), (0, 0)))
    coeff_block = coeff_terms.astype(jnp.bfloat16).reshape(slot_count * rank, rows_all)
    vec_block = vec_padded.reshape(-1, rows_all)
    joined = rep_sum(jnp.concatenate([coeff_block, vec_block], axis=0))
    coeffs = joined[: slot_count * rank].reshape(slot_count, rank, rows_all)
    vec_summed = joined[slot_count * rank:].reshape(vec_padded.shape)[:vec_rows]
    owned_mask = is_owned[:, None, None]
    emb_mask = is_embedding[:, None, None]

    def fresh(start_part, momentum_part, change, basis_cols):
        projected = jnp.einsum("skb,kq->sbq", coeffs, basis_cols, precision=lax.Precision.HIGH)
        outer_grad = jnp.where(emb_mask, projected, change)
        fresh_momentum = outer_momentum * momentum_part + outer_grad
        fresh_start = start_part - outer_rate * (outer_grad + outer_momentum * fresh_momentum)
        return fresh_start, fresh_momentum

    returned = None
    all_changes = jnp.concatenate(changes, axis=2)
    projected_all = jnp.einsum("skb,kq->sbq", coeffs, basis_part, precision=lax.Precision.HIGH)
    grad_all = jnp.where(emb_mask, projected_all, all_changes)
    rounded_all = (held - (outer_rate * (1.0 + outer_momentum)) * grad_all).astype(jnp.bfloat16)
    for c in range(2):
        rounded = rounded_all[:, :, halves[c]]
        if c == 1 and dev_count <= 8:
            me = lax.axis_index("dev")
            part_rows = rounded.shape[1] // dev_count
            blocks = [lax.dynamic_slice_in_dim(rounded, me * part_rows, part_rows, 1)]
            for k in range(1, dev_count):
                out_rows = lax.dynamic_slice_in_dim(rounded, ((me + k) % dev_count) * part_rows, part_rows, 1)
                blocks.append(lax.ppermute(out_rows, "dev", [(i, (i + k) % dev_count) for i in range(dev_count)]))
            pieces = jnp.concatenate(blocks, axis=0)
            shifted = ((me - owner) % dev_count) * slot_count + slot_of
            picked = jnp.take(pieces, shifted, axis=0, mode="clip")
        else:
            pieces = lax.all_to_all(rounded, "dev", split_axis=1, concat_axis=0, tiled=True)
            picked = jnp.take(pieces, target, axis=0, mode="clip")
        gathered = lax.all_gather(picked, "rep", axis=2, tiled=True)
        if c == 0:
            late_inputs = lax.optimization_barrier((start_rows, momentum_rows, changes[0], changes[1], coeffs, gathered))
            gathered = late_inputs[5]
        returned = place_half(gathered, width, c, returned)
    late_start, late_momentum, late_change0, late_change1, late_coeffs, _ = late_inputs
    coeffs = late_coeffs
    fresh_start, fresh_momentum = fresh(late_start, late_momentum, jnp.concatenate([late_change0, late_change1], axis=2), basis_part)
    new_momentum = jnp.where(owned_mask, fresh_momentum, late_momentum)
    new_start = jnp.where(owned_mask, fresh_start, late_start)
    vec_change = vec_start - vec_summed / rep_count
    vec_new_momentum = outer_momentum * vec_momentum + vec_change
    vec_new = vec_start - outer_rate * (vec_change + outer_momentum * vec_new_momentum)
    return (new_start[None], new_momentum[None], returned, vec_new, vec_new_momentum)


def solution(mesh):
    return jax.shard_map(
        body,
        mesh=mesh,
        in_specs=(
            P("rep", None, "dev", None),
            P(),
            P("dev", None, None, "rep"),
            P("dev", None, None, "rep"),
            P(),
            P("rep", None, None),
            P(),
            P(),
        ),
        out_specs=(
            P("dev", None, None, "rep"),
            P("dev", None, None, "rep"),
            P(None, "dev", None),
            P(),
            P(),
        ),
        check_vma=False,
    )
```

```python
import jax
import jax.numpy as jnp
from jax import lax
from jax.sharding import PartitionSpec as P
from jax.experimental import pallas as pl

EMB_FIRST = 96


outer_rate = 0.7
outer_momentum = 0.9


def rep_sum(x):
    rep_count = lax.axis_size("rep")
    if rep_count != 4:
        total = x.astype(jnp.bfloat16)
        step = 1
        while step < rep_count:
            other = lax.ppermute(total, "rep", [(i, i ^ step) for i in range(rep_count)])
            total = total.astype(jnp.float32) + other.astype(jnp.float32)
            step *= 2
            if step < rep_count:
                total = total.astype(jnp.bfloat16)
        return total
    core = lax.axis_index("rep") % 2
    mine = x.astype(jnp.bfloat16)
    other = lax.ppermute(mine, "rep", [(i, i ^ 1) for i in range(4)])
    pair = (mine.astype(jnp.float32) + other.astype(jnp.float32)).astype(jnp.bfloat16)
    pair = pair.reshape((2, x.shape[0] // 2) + x.shape[1:])
    part = lax.dynamic_index_in_dim(pair, core, 0, keepdims=False)
    across = lax.ppermute(part, "rep", [(i, i ^ 2) for i in range(4)])
    done = part.astype(jnp.float32) + across.astype(jnp.float32)
    rest = lax.ppermute(done, "rep", [(i, i ^ 1) for i in range(4)])
    first = jnp.where(core == 0, done, rest)
    second = jnp.where(core == 0, rest, done)
    return jnp.concatenate([first, second], axis=0)


def _copy_kernel(x_ref, o_ref):
    o_ref[...] = x_ref[...].reshape(o_ref.shape)


def take_half(x, width, half):
    units, rows, full = x.shape
    quarters = full // (2 * width)
    return pl.pallas_call(
        _copy_kernel,
        grid=(quarters,),
        in_specs=[pl.BlockSpec((units, rows, width), lambda q: (0, 0, 2 * q + half))],
        out_specs=pl.BlockSpec((1, units, rows, width), lambda q: (q, 0, 0, 0)),
        out_shape=jax.ShapeDtypeStruct((quarters, units, rows, width), x.dtype),
    )(x)


def _place_kernel(a_ref, base_ref, o_ref):
    del base_ref
    o_ref[...] = a_ref[...]


def place_half(a, width, half, base=None):
    units, rows, part = a.shape
    quarters = part // width
    in_spec = pl.BlockSpec((units, rows, width), lambda q: (0, 0, q))
    out_spec = pl.BlockSpec((units, rows, width), lambda q: (0, 0, 2 * q + half))
    out_shape = jax.ShapeDtypeStruct((units, rows, 2 * part), a.dtype)
    if base is None:
        return pl.pallas_call(
            _copy_kernel, grid=(quarters,), in_specs=[in_spec], out_specs=out_spec, out_shape=out_shape
        )(a)
    return pl.pallas_call(
        _place_kernel,
        grid=(quarters,),
        in_specs=[in_spec, pl.BlockSpec(memory_space=pl.ANY)],
        out_specs=out_spec,
        out_shape=out_shape,
        input_output_aliases={1: 0},
    )(a, base)


def body(group_weights, owner, start_weights, momentum, basis, vec_groups, vec_start, vec_momentum):
    dev_count = lax.axis_size("dev")
    rep_count = lax.axis_size("rep")
    unit_count = owner.shape[0]
    slot_count = start_weights.shape[1]
    quarter = start_weights.shape[3]
    unit_ids = jnp.arange(unit_count, dtype=jnp.int32)
    same_owner = owner[:, None] == owner[None, :]
    earlier = unit_ids[None, :] < unit_ids[:, None]
    slot_of = jnp.sum((same_owner & earlier).astype(jnp.int32), axis=1)
    target = owner * slot_count + slot_of
    positions = jnp.arange(dev_count * slot_count, dtype=jnp.int32)
    placed = target[:, None] == positions[None, :]
    source_unit = jnp.sum(jnp.where(placed, unit_ids[:, None], 0), axis=0)
    own_rows = group_weights[0]
    width = quarter // 2
    start_rows = start_weights[0]
    momentum_rows = momentum[0]
    my_slots = lax.axis_index("dev") * slot_count + jnp.arange(slot_count, dtype=jnp.int32)
    own_placed = target[:, None] == my_slots[None, :]
    is_owned = jnp.any(own_placed, axis=0)
    is_embedding = jnp.any(own_placed & (unit_ids >= EMB_FIRST)[:, None], axis=0)
    first_column = lax.axis_index("rep") * quarter
    basis_part = lax.dynamic_slice_in_dim(basis, first_column, quarter, 1)
    halves = [slice(c * width, (c + 1) * width) for c in range(2)]
    held = start_rows - (outer_rate * outer_momentum * outer_momentum) * momentum_rows
    changes = []
    coeff_terms = None
    for c in range(2):
        half = take_half(own_rows, width, c)
        summed = lax.psum_scatter(half, "rep", scatter_dimension=0, tiled=True)[0]
        picked = jnp.take(summed, source_unit, axis=0, mode="clip")
        arrived = lax.all_to_all(
            picked.reshape(dev_count, slot_count, summed.shape[1], summed.shape[2]),
            "dev",
            split_axis=0,
            concat_axis=2,
            tiled=True,
        )
        change = start_rows[:, :, halves[c]] - arrived[0].astype(jnp.float32) / rep_count
        changes.append(change)
        term = jnp.einsum("sbq,kq->skb", change, basis_part[:, halves[c]], precision=lax.Precision.HIGH)
        coeff_terms = term if coeff_terms is None else coeff_terms + term
    rank = coeff_terms.shape[1]
    rows_all = coeff_terms.shape[2]
    vec_terms = vec_groups[0]
    vec_rows = vec_terms.shape[0]
    vec_padded = jnp.pad(vec_terms, ((0, (-vec_rows) % 16), (0, 0)))
    coeff_block = coeff_terms.astype(jnp.bfloat16).reshape(slot_count * rank, rows_all)
    vec_block = vec_padded.reshape(-1, rows_all)
    joined = rep_sum(jnp.concatenate([coeff_block, vec_block], axis=0))
    coeffs = joined[: slot_count * rank].reshape(slot_count, rank, rows_all)
    vec_summed = joined[slot_count * rank:].reshape(vec_padded.shape)[:vec_rows]
    owned_mask = is_owned[:, None, None]
    emb_mask = is_embedding[:, None, None]

    def fresh(start_part, momentum_part, change, basis_cols):
        projected = jnp.einsum("skb,kq->sbq", coeffs, basis_cols, precision=lax.Precision.HIGH)
        outer_grad = jnp.where(emb_mask, projected, change)
        fresh_momentum = outer_momentum * momentum_part + outer_grad
        fresh_start = start_part - outer_rate * (outer_grad + outer_momentum * fresh_momentum)
        return fresh_start, fresh_momentum

    returned = None
    all_changes = jnp.concatenate(changes, axis=2)
    projected_all = jnp.einsum("skb,kq->sbq", coeffs, basis_part, precision=lax.Precision.HIGH)
    grad_all = jnp.where(emb_mask, projected_all, all_changes)
    rounded_all = (held - (outer_rate * (1.0 + outer_momentum)) * grad_all).astype(jnp.bfloat16)
    for c in range(2):
        rounded = rounded_all[:, :, halves[c]]
        if dev_count <= 8:
            me = lax.axis_index("dev")
            part_rows = rounded.shape[1] // dev_count
            blocks = [lax.dynamic_slice_in_dim(rounded, me * part_rows, part_rows, 1)]
            for k in range(1, dev_count):
                out_rows = lax.dynamic_slice_in_dim(rounded, ((me + k) % dev_count) * part_rows, part_rows, 1)
                blocks.append(lax.ppermute(out_rows, "dev", [(i, (i + k) % dev_count) for i in range(dev_count)]))
            pieces = jnp.concatenate(blocks, axis=0)
            shifted = ((me - owner) % dev_count) * slot_count + slot_of
            picked = jnp.take(pieces, shifted, axis=0, mode="clip")
        else:
            pieces = lax.all_to_all(rounded, "dev", split_axis=1, concat_axis=0, tiled=True)
            picked = jnp.take(pieces, target, axis=0, mode="clip")
        gathered = lax.all_gather(picked, "rep", axis=2, tiled=True)
        if c == 0:
            late_inputs = lax.optimization_barrier((start_rows, momentum_rows, changes[0], changes[1], coeffs, gathered))
            gathered = late_inputs[5]
        returned = place_half(gathered, width, c, returned)
    late_start, late_momentum, late_change0, late_change1, late_coeffs, _ = late_inputs
    coeffs = late_coeffs
    fresh_start, fresh_momentum = fresh(late_start, late_momentum, jnp.concatenate([late_change0, late_change1], axis=2), basis_part)
    new_momentum = jnp.where(owned_mask, fresh_momentum, late_momentum)
    new_start = jnp.where(owned_mask, fresh_start, late_start)
    vec_change = vec_start - vec_summed / rep_count
    vec_new_momentum = outer_momentum * vec_momentum + vec_change
    vec_new = vec_start - outer_rate * (vec_change + outer_momentum * vec_new_momentum)
    return (new_start[None], new_momentum[None], returned, vec_new, vec_new_momentum)


def solution(mesh):
    return jax.shard_map(
        body,
        mesh=mesh,
        in_specs=(
            P("rep", None, "dev", None),
            P(),
            P("dev", None, None, "rep"),
            P("dev", None, None, "rep"),
            P(),
            P("rep", None, None),
            P(),
            P(),
        ),
        out_specs=(
            P("dev", None, None, "rep"),
            P("dev", None, None, "rep"),
            P(None, "dev", None),
            P(),
            P(),
        ),
        check_vma=False,
    )
```

```python
import jax
import jax.numpy as jnp
from jax import lax
from jax.sharding import PartitionSpec as P
from jax.experimental import pallas as pl

EMB_FIRST = 96


outer_rate = 0.7
outer_momentum = 0.9


def rep_sum(x):
    rep_count = lax.axis_size("rep")
    if rep_count != 4:
        total = x.astype(jnp.bfloat16)
        step = 1
        while step < rep_count:
            other = lax.ppermute(total, "rep", [(i, i ^ step) for i in range(rep_count)])
            total = total.astype(jnp.float32) + other.astype(jnp.float32)
            step *= 2
            if step < rep_count:
                total = total.astype(jnp.bfloat16)
        return total
    core = lax.axis_index("rep") % 2
    mine = x.astype(jnp.bfloat16)
    other = lax.ppermute(mine, "rep", [(i, i ^ 1) for i in range(4)])
    pair = (mine.astype(jnp.float32) + other.astype(jnp.float32)).astype(jnp.bfloat16)
    pair = pair.reshape((2, x.shape[0] // 2) + x.shape[1:])
    part = lax.dynamic_index_in_dim(pair, core, 0, keepdims=False)
    across = lax.ppermute(part, "rep", [(i, i ^ 2) for i in range(4)])
    done = part.astype(jnp.float32) + across.astype(jnp.float32)
    rest = lax.ppermute(done, "rep", [(i, i ^ 1) for i in range(4)])
    first = jnp.where(core == 0, done, rest)
    second = jnp.where(core == 0, rest, done)
    return jnp.concatenate([first, second], axis=0)


def _copy_kernel(x_ref, o_ref):
    o_ref[...] = x_ref[...].reshape(o_ref.shape)


def take_half(x, width, half):
    units, rows, full = x.shape
    quarters = full // (2 * width)
    return pl.pallas_call(
        _copy_kernel,
        grid=(quarters,),
        in_specs=[pl.BlockSpec((units, rows, width), lambda q: (0, 0, 2 * q + half))],
        out_specs=pl.BlockSpec((1, units, rows, width), lambda q: (q, 0, 0, 0)),
        out_shape=jax.ShapeDtypeStruct((quarters, units, rows, width), x.dtype),
    )(x)


def _place_kernel(a_ref, base_ref, o_ref):
    del base_ref
    o_ref[...] = a_ref[...]


def place_half(a, width, half, base=None):
    units, rows, part = a.shape
    quarters = part // width
    in_spec = pl.BlockSpec((units, rows, width), lambda q: (0, 0, q))
    out_spec = pl.BlockSpec((units, rows, width), lambda q: (0, 0, 2 * q + half))
    out_shape = jax.ShapeDtypeStruct((units, rows, 2 * part), a.dtype)
    if base is None:
        return pl.pallas_call(
            _copy_kernel, grid=(quarters,), in_specs=[in_spec], out_specs=out_spec, out_shape=out_shape
        )(a)
    return pl.pallas_call(
        _place_kernel,
        grid=(quarters,),
        in_specs=[in_spec, pl.BlockSpec(memory_space=pl.ANY)],
        out_specs=out_spec,
        out_shape=out_shape,
        input_output_aliases={1: 0},
    )(a, base)


def body(group_weights, owner, start_weights, momentum, basis, vec_groups, vec_start, vec_momentum):
    dev_count = lax.axis_size("dev")
    rep_count = lax.axis_size("rep")
    unit_count = owner.shape[0]
    slot_count = start_weights.shape[1]
    quarter = start_weights.shape[3]
    unit_ids = jnp.arange(unit_count, dtype=jnp.int32)
    same_owner = owner[:, None] == owner[None, :]
    earlier = unit_ids[None, :] < unit_ids[:, None]
    slot_of = jnp.sum((same_owner & earlier).astype(jnp.int32), axis=1)
    target = owner * slot_count + slot_of
    positions = jnp.arange(dev_count * slot_count, dtype=jnp.int32)
    placed = target[:, None] == positions[None, :]
    source_unit = jnp.sum(jnp.where(placed, unit_ids[:, None], 0), axis=0)
    own_rows = group_weights[0]
    width = quarter // 2
    start_rows = start_weights[0]
    momentum_rows = momentum[0]
    my_slots = lax.axis_index("dev") * slot_count + jnp.arange(slot_count, dtype=jnp.int32)
    own_placed = target[:, None] == my_slots[None, :]
    is_owned = jnp.any(own_placed, axis=0)
    is_embedding = jnp.any(own_placed & (unit_ids >= EMB_FIRST)[:, None], axis=0)
    first_column = lax.axis_index("rep") * quarter
    basis_part = lax.dynamic_slice_in_dim(basis, first_column, quarter, 1)
    halves = [slice(c * width, (c + 1) * width) for c in range(2)]
    held = start_rows - (outer_rate * outer_momentum * outer_momentum) * momentum_rows
    changes = []
    coeff_terms = None
    for c in range(2):
        half = take_half(own_rows, width, c)
        summed = lax.psum_scatter(half, "rep", scatter_dimension=0, tiled=True)[0]
        if c == 1 and dev_count <= 8:
            me = lax.axis_index("dev")
            part_rows = summed.shape[1]
            arrived = jnp.zeros((slot_count, dev_count * part_rows, width), summed.dtype)
            for k in range(dev_count):
                dest = (me + k) % dev_count
                units = lax.dynamic_slice_in_dim(source_unit, dest * slot_count, slot_count)
                block = jnp.take(summed, units, axis=0, mode="clip")
                if k:
                    block = lax.ppermute(block, "dev", [(i, (i + k) % dev_count) for i in range(dev_count)])
                arrived = lax.dynamic_update_slice_in_dim(arrived, block, ((me - k) % dev_count) * part_rows, 1)
        else:
            picked = jnp.take(summed, source_unit, axis=0, mode="clip")
            arrived = lax.all_to_all(
                picked.reshape(dev_count, slot_count, summed.shape[1], summed.shape[2]),
                "dev",
                split_axis=0,
                concat_axis=2,
                tiled=True,
            )[0]
        change = start_rows[:, :, halves[c]] - arrived.astype(jnp.float32) / rep_count
        changes.append(change)
        term = jnp.einsum("sbq,kq->skb", change, basis_part[:, halves[c]], precision=lax.Precision.HIGH)
        coeff_terms = term if coeff_terms is None else coeff_terms + term
    rank = coeff_terms.shape[1]
    rows_all = coeff_terms.shape[2]
    vec_terms = vec_groups[0]
    vec_rows = vec_terms.shape[0]
    vec_padded = jnp.pad(vec_terms, ((0, (-vec_rows) % 16), (0, 0)))
    coeff_block = coeff_terms.astype(jnp.bfloat16).reshape(slot_count * rank, rows_all)
    vec_block = vec_padded.reshape(-1, rows_all)
    joined = rep_sum(jnp.concatenate([coeff_block, vec_block], axis=0))
    coeffs = joined[: slot_count * rank].reshape(slot_count, rank, rows_all)
    vec_summed = joined[slot_count * rank:].reshape(vec_padded.shape)[:vec_rows]
    owned_mask = is_owned[:, None, None]
    emb_mask = is_embedding[:, None, None]

    def fresh(start_part, momentum_part, change, basis_cols):
        projected = jnp.einsum("skb,kq->sbq", coeffs, basis_cols, precision=lax.Precision.HIGH)
        outer_grad = jnp.where(emb_mask, projected, change)
        fresh_momentum = outer_momentum * momentum_part + outer_grad
        fresh_start = start_part - outer_rate * (outer_grad + outer_momentum * fresh_momentum)
        return fresh_start, fresh_momentum

    returned = None
    all_changes = jnp.concatenate(changes, axis=2)
    projected_all = jnp.einsum("skb,kq->sbq", coeffs, basis_part, precision=lax.Precision.HIGH)
    grad_all = jnp.where(emb_mask, projected_all, all_changes)
    rounded_all = (held - (outer_rate * (1.0 + outer_momentum)) * grad_all).astype(jnp.bfloat16)
    for c in range(2):
        rounded = rounded_all[:, :, halves[c]]
        if dev_count <= 8:
            me = lax.axis_index("dev")
            part_rows = rounded.shape[1] // dev_count
            blocks = [lax.dynamic_slice_in_dim(rounded, me * part_rows, part_rows, 1)]
            for k in range(1, dev_count):
                out_rows = lax.dynamic_slice_in_dim(rounded, ((me + k) % dev_count) * part_rows, part_rows, 1)
                blocks.append(lax.ppermute(out_rows, "dev", [(i, (i + k) % dev_count) for i in range(dev_count)]))
            pieces = jnp.concatenate(blocks, axis=0)
            shifted = ((me - owner) % dev_count) * slot_count + slot_of
            picked = jnp.take(pieces, shifted, axis=0, mode="clip")
        else:
            pieces = lax.all_to_all(rounded, "dev", split_axis=1, concat_axis=0, tiled=True)
            picked = jnp.take(pieces, target, axis=0, mode="clip")
        gathered = lax.all_gather(picked, "rep", axis=2, tiled=True)
        if c == 0:
            late_inputs = lax.optimization_barrier((start_rows, momentum_rows, changes[0], changes[1], coeffs, gathered))
            gathered = late_inputs[5]
        returned = place_half(gathered, width, c, returned)
    late_start, late_momentum, late_change0, late_change1, late_coeffs, _ = late_inputs
    coeffs = late_coeffs
    fresh_start, fresh_momentum = fresh(late_start, late_momentum, jnp.concatenate([late_change0, late_change1], axis=2), basis_part)
    new_momentum = jnp.where(owned_mask, fresh_momentum, late_momentum)
    new_start = jnp.where(owned_mask, fresh_start, late_start)
    vec_change = vec_start - vec_summed / rep_count
    vec_new_momentum = outer_momentum * vec_momentum + vec_change
    vec_new = vec_start - outer_rate * (vec_change + outer_momentum * vec_new_momentum)
    return (new_start[None], new_momentum[None], returned, vec_new, vec_new_momentum)


def solution(mesh):
    return jax.shard_map(
        body,
        mesh=mesh,
        in_specs=(
            P("rep", None, "dev", None),
            P(),
            P("dev", None, None, "rep"),
            P("dev", None, None, "rep"),
            P(),
            P("rep", None, None),
            P(),
            P(),
        ),
        out_specs=(
            P("dev", None, None, "rep"),
            P("dev", None, None, "rep"),
            P(None, "dev", None),
            P(),
            P(),
        ),
        check_vma=False,
    )
```

```python
import jax
import jax.numpy as jnp
from jax import lax
from jax.sharding import PartitionSpec as P
from jax.experimental import pallas as pl

EMB_FIRST = 96


outer_rate = 0.7
outer_momentum = 0.9


def rep_sum(x):
    rep_count = lax.axis_size("rep")
    if rep_count != 4:
        total = x.astype(jnp.bfloat16)
        step = 1
        while step < rep_count:
            other = lax.ppermute(total, "rep", [(i, i ^ step) for i in range(rep_count)])
            total = total.astype(jnp.float32) + other.astype(jnp.float32)
            step *= 2
            if step < rep_count:
                total = total.astype(jnp.bfloat16)
        return total
    core = lax.axis_index("rep") % 2
    mine = x.astype(jnp.bfloat16)
    other = lax.ppermute(mine, "rep", [(i, i ^ 1) for i in range(4)])
    pair = (mine.astype(jnp.float32) + other.astype(jnp.float32)).astype(jnp.bfloat16)
    pair = pair.reshape((2, x.shape[0] // 2) + x.shape[1:])
    part = lax.dynamic_index_in_dim(pair, core, 0, keepdims=False)
    across = lax.ppermute(part, "rep", [(i, i ^ 2) for i in range(4)])
    done = part.astype(jnp.float32) + across.astype(jnp.float32)
    rest = lax.ppermute(done, "rep", [(i, i ^ 1) for i in range(4)])
    first = jnp.where(core == 0, done, rest)
    second = jnp.where(core == 0, rest, done)
    return jnp.concatenate([first, second], axis=0)


def _copy_kernel(x_ref, o_ref):
    o_ref[...] = x_ref[...].reshape(o_ref.shape)


def take_half(x, width, half):
    units, rows, full = x.shape
    quarters = full // (2 * width)
    return pl.pallas_call(
        _copy_kernel,
        grid=(quarters,),
        in_specs=[pl.BlockSpec((units, rows, width), lambda q: (0, 0, 2 * q + half))],
        out_specs=pl.BlockSpec((1, units, rows, width), lambda q: (q, 0, 0, 0)),
        out_shape=jax.ShapeDtypeStruct((quarters, units, rows, width), x.dtype),
    )(x)


def _place_kernel(a_ref, base_ref, o_ref):
    del base_ref
    o_ref[...] = a_ref[...]


def place_half(a, width, half, base=None):
    units, rows, part = a.shape
    quarters = part // width
    in_spec = pl.BlockSpec((units, rows, width), lambda q: (0, 0, q))
    out_spec = pl.BlockSpec((units, rows, width), lambda q: (0, 0, 2 * q + half))
    out_shape = jax.ShapeDtypeStruct((units, rows, 2 * part), a.dtype)
    if base is None:
        return pl.pallas_call(
            _copy_kernel, grid=(quarters,), in_specs=[in_spec], out_specs=out_spec, out_shape=out_shape
        )(a)
    return pl.pallas_call(
        _place_kernel,
        grid=(quarters,),
        in_specs=[in_spec, pl.BlockSpec(memory_space=pl.ANY)],
        out_specs=out_spec,
        out_shape=out_shape,
        input_output_aliases={1: 0},
    )(a, base)


def body(group_weights, owner, start_weights, momentum, basis, vec_groups, vec_start, vec_momentum):
    dev_count = lax.axis_size("dev")
    rep_count = lax.axis_size("rep")
    unit_count = owner.shape[0]
    slot_count = start_weights.shape[1]
    quarter = start_weights.shape[3]
    unit_ids = jnp.arange(unit_count, dtype=jnp.int32)
    same_owner = owner[:, None] == owner[None, :]
    earlier = unit_ids[None, :] < unit_ids[:, None]
    slot_of = jnp.sum((same_owner & earlier).astype(jnp.int32), axis=1)
    target = owner * slot_count + slot_of
    positions = jnp.arange(dev_count * slot_count, dtype=jnp.int32)
    placed = target[:, None] == positions[None, :]
    source_unit = jnp.sum(jnp.where(placed, unit_ids[:, None], 0), axis=0)
    own_rows = group_weights[0]
    width = quarter // 2
    start_rows = start_weights[0]
    momentum_rows = momentum[0]
    my_slots = lax.axis_index("dev") * slot_count + jnp.arange(slot_count, dtype=jnp.int32)
    own_placed = target[:, None] == my_slots[None, :]
    is_owned = jnp.any(own_placed, axis=0)
    is_embedding = jnp.any(own_placed & (unit_ids >= EMB_FIRST)[:, None], axis=0)
    first_column = lax.axis_index("rep") * quarter
    basis_part = lax.dynamic_slice_in_dim(basis, first_column, quarter, 1)
    halves = [slice(c * width, (c + 1) * width) for c in range(2)]
    held = start_rows - (outer_rate * outer_momentum * outer_momentum) * momentum_rows
    changes = []
    coeff_terms = None
    for c in range(2):
        half = take_half(own_rows, width, c)
        summed = lax.psum_scatter(half, "rep", scatter_dimension=0, tiled=True)[0]
        if c == 1 and dev_count <= 8:
            me = lax.axis_index("dev")
            part_rows = summed.shape[1]
            arrived = jnp.zeros((slot_count, dev_count * part_rows, width), summed.dtype)
            picked = jnp.take(summed, source_unit, axis=0, mode="clip").reshape(dev_count, slot_count, part_rows, width)
            for k in range(dev_count):
                block = lax.dynamic_index_in_dim(picked, (me + k) % dev_count, 0, keepdims=False)
                if k:
                    block = lax.ppermute(block, "dev", [(i, (i + k) % dev_count) for i in range(dev_count)])
                arrived = lax.dynamic_update_slice_in_dim(arrived, block, ((me - k) % dev_count) * part_rows, 1)
        else:
            picked = jnp.take(summed, source_unit, axis=0, mode="clip")
            arrived = lax.all_to_all(
                picked.reshape(dev_count, slot_count, summed.shape[1], summed.shape[2]),
                "dev",
                split_axis=0,
                concat_axis=2,
                tiled=True,
            )[0]
        change = start_rows[:, :, halves[c]] - arrived.astype(jnp.float32) / rep_count
        changes.append(change)
        term = jnp.einsum("sbq,kq->skb", change, basis_part[:, halves[c]], precision=lax.Precision.HIGH)
        coeff_terms = term if coeff_terms is None else coeff_terms + term
    rank = coeff_terms.shape[1]
    rows_all = coeff_terms.shape[2]
    vec_terms = vec_groups[0]
    vec_rows = vec_terms.shape[0]
    vec_padded = jnp.pad(vec_terms, ((0, (-vec_rows) % 16), (0, 0)))
    coeff_block = coeff_terms.astype(jnp.bfloat16).reshape(slot_count * rank, rows_all)
    vec_block = vec_padded.reshape(-1, rows_all)
    joined = rep_sum(jnp.concatenate([coeff_block, vec_block], axis=0))
    coeffs = joined[: slot_count * rank].reshape(slot_count, rank, rows_all)
    vec_summed = joined[slot_count * rank:].reshape(vec_padded.shape)[:vec_rows]
    owned_mask = is_owned[:, None, None]
    emb_mask = is_embedding[:, None, None]

    def fresh(start_part, momentum_part, change, basis_cols):
        projected = jnp.einsum("skb,kq->sbq", coeffs, basis_cols, precision=lax.Precision.HIGH)
        outer_grad = jnp.where(emb_mask, projected, change)
        fresh_momentum = outer_momentum * momentum_part + outer_grad
        fresh_start = start_part - outer_rate * (outer_grad + outer_momentum * fresh_momentum)
        return fresh_start, fresh_momentum

    returned = None
    all_changes = jnp.concatenate(changes, axis=2)
    projected_all = jnp.einsum("skb,kq->sbq", coeffs, basis_part, precision=lax.Precision.HIGH)
    grad_all = jnp.where(emb_mask, projected_all, all_changes)
    rounded_all = (held - (outer_rate * (1.0 + outer_momentum)) * grad_all).astype(jnp.bfloat16)
    for c in range(2):
        rounded = rounded_all[:, :, halves[c]]
        if dev_count <= 8:
            me = lax.axis_index("dev")
            part_rows = rounded.shape[1] // dev_count
            blocks = [lax.dynamic_slice_in_dim(rounded, me * part_rows, part_rows, 1)]
            for k in range(1, dev_count):
                out_rows = lax.dynamic_slice_in_dim(rounded, ((me + k) % dev_count) * part_rows, part_rows, 1)
                blocks.append(lax.ppermute(out_rows, "dev", [(i, (i + k) % dev_count) for i in range(dev_count)]))
            pieces = jnp.concatenate(blocks, axis=0)
            shifted = ((me - owner) % dev_count) * slot_count + slot_of
            picked = jnp.take(pieces, shifted, axis=0, mode="clip")
        else:
            pieces = lax.all_to_all(rounded, "dev", split_axis=1, concat_axis=0, tiled=True)
            picked = jnp.take(pieces, target, axis=0, mode="clip")
        gathered = lax.all_gather(picked, "rep", axis=2, tiled=True)
        if c == 0:
            late_inputs = lax.optimization_barrier((start_rows, momentum_rows, changes[0], changes[1], coeffs, gathered))
            gathered = late_inputs[5]
        returned = place_half(gathered, width, c, returned)
    late_start, late_momentum, late_change0, late_change1, late_coeffs, _ = late_inputs
    coeffs = late_coeffs
    fresh_start, fresh_momentum = fresh(late_start, late_momentum, jnp.concatenate([late_change0, late_change1], axis=2), basis_part)
    new_momentum = jnp.where(owned_mask, fresh_momentum, late_momentum)
    new_start = jnp.where(owned_mask, fresh_start, late_start)
    vec_change = vec_start - vec_summed / rep_count
    vec_new_momentum = outer_momentum * vec_momentum + vec_change
    vec_new = vec_start - outer_rate * (vec_change + outer_momentum * vec_new_momentum)
    return (new_start[None], new_momentum[None], returned, vec_new, vec_new_momentum)


def solution(mesh):
    return jax.shard_map(
        body,
        mesh=mesh,
        in_specs=(
            P("rep", None, "dev", None),
            P(),
            P("dev", None, None, "rep"),
            P("dev", None, None, "rep"),
            P(),
            P("rep", None, None),
            P(),
            P(),
        ),
        out_specs=(
            P("dev", None, None, "rep"),
            P("dev", None, None, "rep"),
            P(None, "dev", None),
            P(),
            P(),
        ),
        check_vma=False,
    )
```

```python
import functools

import jax
import jax.numpy as jnp
from jax import lax
from jax.sharding import PartitionSpec as P
from jax.experimental import pallas as pl

EMB_FIRST = 96


outer_rate = 0.7
outer_momentum = 0.9


def rep_sum(x):
    rep_count = lax.axis_size("rep")
    if rep_count != 4:
        total = x.astype(jnp.bfloat16)
        step = 1
        while step < rep_count:
            other = lax.ppermute(total, "rep", [(i, i ^ step) for i in range(rep_count)])
            total = total.astype(jnp.float32) + other.astype(jnp.float32)
            step *= 2
            if step < rep_count:
                total = total.astype(jnp.bfloat16)
        return total
    core = lax.axis_index("rep") % 2
    mine = x.astype(jnp.bfloat16)
    other = lax.ppermute(mine, "rep", [(i, i ^ 1) for i in range(4)])
    pair = (mine.astype(jnp.float32) + other.astype(jnp.float32)).astype(jnp.bfloat16)
    pair = pair.reshape((2, x.shape[0] // 2) + x.shape[1:])
    part = lax.dynamic_index_in_dim(pair, core, 0, keepdims=False)
    across = lax.ppermute(part, "rep", [(i, i ^ 2) for i in range(4)])
    done = part.astype(jnp.float32) + across.astype(jnp.float32)
    rest = lax.ppermute(done, "rep", [(i, i ^ 1) for i in range(4)])
    first = jnp.where(core == 0, done, rest)
    second = jnp.where(core == 0, rest, done)
    return jnp.concatenate([first, second], axis=0)


def _copy_kernel(x_ref, o_ref):
    o_ref[...] = x_ref[...].reshape(o_ref.shape)


def _half_kernel(half, x_ref, o_ref):
    w = o_ref.shape[-1]
    for q in range(o_ref.shape[0]):
        o_ref[q] = x_ref[:, :, (2 * q + half) * w:(2 * q + half + 1) * w]


def take_half(x, width, half):
    units, rows, full = x.shape
    quarters = full // (2 * width)
    step = units // 4 if units % 32 == 0 else units
    return pl.pallas_call(
        functools.partial(_half_kernel, half),
        grid=(units // step,),
        in_specs=[pl.BlockSpec((step, rows, full), lambda i: (i, 0, 0))],
        out_specs=pl.BlockSpec((quarters, step, rows, width), lambda i: (0, i, 0, 0)),
        out_shape=jax.ShapeDtypeStruct((quarters, units, rows, width), x.dtype),
    )(x)


def _place_kernel(a_ref, base_ref, o_ref):
    del base_ref
    o_ref[...] = a_ref[...]


def place_half(a, width, half, base=None):
    units, rows, part = a.shape
    quarters = part // width
    in_spec = pl.BlockSpec((units, rows, width), lambda q: (0, 0, q))
    out_spec = pl.BlockSpec((units, rows, width), lambda q: (0, 0, 2 * q + half))
    out_shape = jax.ShapeDtypeStruct((units, rows, 2 * part), a.dtype)
    if base is None:
        return pl.pallas_call(
            _copy_kernel, grid=(quarters,), in_specs=[in_spec], out_specs=out_spec, out_shape=out_shape
        )(a)
    return pl.pallas_call(
        _place_kernel,
        grid=(quarters,),
        in_specs=[in_spec, pl.BlockSpec(memory_space=pl.ANY)],
        out_specs=out_spec,
        out_shape=out_shape,
        input_output_aliases={1: 0},
    )(a, base)


def body(group_weights, owner, start_weights, momentum, basis, vec_groups, vec_start, vec_momentum):
    dev_count = lax.axis_size("dev")
    rep_count = lax.axis_size("rep")
    unit_count = owner.shape[0]
    slot_count = start_weights.shape[1]
    quarter = start_weights.shape[3]
    unit_ids = jnp.arange(unit_count, dtype=jnp.int32)
    same_owner = owner[:, None] == owner[None, :]
    earlier = unit_ids[None, :] < unit_ids[:, None]
    slot_of = jnp.sum((same_owner & earlier).astype(jnp.int32), axis=1)
    target = owner * slot_count + slot_of
    positions = jnp.arange(dev_count * slot_count, dtype=jnp.int32)
    placed = target[:, None] == positions[None, :]
    source_unit = jnp.sum(jnp.where(placed, unit_ids[:, None], 0), axis=0)
    own_rows = group_weights[0]
    width = quarter // 2
    start_rows = start_weights[0]
    momentum_rows = momentum[0]
    my_slots = lax.axis_index("dev") * slot_count + jnp.arange(slot_count, dtype=jnp.int32)
    own_placed = target[:, None] == my_slots[None, :]
    is_owned = jnp.any(own_placed, axis=0)
    is_embedding = jnp.any(own_placed & (unit_ids >= EMB_FIRST)[:, None], axis=0)
    first_column = lax.axis_index("rep") * quarter
    basis_part = lax.dynamic_slice_in_dim(basis, first_column, quarter, 1)
    halves = [slice(c * width, (c + 1) * width) for c in range(2)]
    held = start_rows - (outer_rate * outer_momentum * outer_momentum) * momentum_rows
    changes = []
    coeff_terms = None
    for c in range(2):
        half = take_half(own_rows, width, c)
        summed = lax.psum_scatter(half, "rep", scatter_dimension=0, tiled=True)[0]
        if c == 1 and dev_count <= 8:
            me = lax.axis_index("dev")
            part_rows = summed.shape[1]
            arrived = jnp.zeros((slot_count, dev_count * part_rows, width), summed.dtype)
            picked = jnp.take(summed, source_unit, axis=0, mode="clip").reshape(dev_count, slot_count, part_rows, width)
            for k in range(dev_count):
                block = lax.dynamic_index_in_dim(picked, (me + k) % dev_count, 0, keepdims=False)
                if k:
                    block = lax.ppermute(block, "dev", [(i, (i + k) % dev_count) for i in range(dev_count)])
                arrived = lax.dynamic_update_slice_in_dim(arrived, block, ((me - k) % dev_count) * part_rows, 1)
        else:
            picked = jnp.take(summed, source_unit, axis=0, mode="clip")
            arrived = lax.all_to_all(
                picked.reshape(dev_count, slot_count, summed.shape[1], summed.shape[2]),
                "dev",
                split_axis=0,
                concat_axis=2,
                tiled=True,
            )[0]
        change = start_rows[:, :, halves[c]] - arrived.astype(jnp.float32) / rep_count
        changes.append(change)
        term = jnp.einsum("sbq,kq->skb", change, basis_part[:, halves[c]], precision=lax.Precision.HIGH)
        coeff_terms = term if coeff_terms is None else coeff_terms + term
    rank = coeff_terms.shape[1]
    rows_all = coeff_terms.shape[2]
    vec_terms = vec_groups[0]
    vec_rows = vec_terms.shape[0]
    vec_padded = jnp.pad(vec_terms, ((0, (-vec_rows) % 16), (0, 0)))
    coeff_block = coeff_terms.astype(jnp.bfloat16).reshape(slot_count * rank, rows_all)
    vec_block = vec_padded.reshape(-1, rows_all)
    joined = rep_sum(jnp.concatenate([coeff_block, vec_block], axis=0))
    coeffs = joined[: slot_count * rank].reshape(slot_count, rank, rows_all)
    vec_summed = joined[slot_count * rank:].reshape(vec_padded.shape)[:vec_rows]
    owned_mask = is_owned[:, None, None]
    emb_mask = is_embedding[:, None, None]

    def fresh(start_part, momentum_part, change, basis_cols):
        projected = jnp.einsum("skb,kq->sbq", coeffs, basis_cols, precision=lax.Precision.HIGH)
        outer_grad = jnp.where(emb_mask, projected, change)
        fresh_momentum = outer_momentum * momentum_part + outer_grad
        fresh_start = start_part - outer_rate * (outer_grad + outer_momentum * fresh_momentum)
        return fresh_start, fresh_momentum

    returned = None
    all_changes = jnp.concatenate(changes, axis=2)
    projected_all = jnp.einsum("skb,kq->sbq", coeffs, basis_part, precision=lax.Precision.HIGH)
    grad_all = jnp.where(emb_mask, projected_all, all_changes)
    rounded_all = (held - (outer_rate * (1.0 + outer_momentum)) * grad_all).astype(jnp.bfloat16)
    for c in range(2):
        rounded = rounded_all[:, :, halves[c]]
        if dev_count <= 8:
            me = lax.axis_index("dev")
            part_rows = rounded.shape[1] // dev_count
            blocks = [lax.dynamic_slice_in_dim(rounded, me * part_rows, part_rows, 1)]
            for k in range(1, dev_count):
                out_rows = lax.dynamic_slice_in_dim(rounded, ((me + k) % dev_count) * part_rows, part_rows, 1)
                blocks.append(lax.ppermute(out_rows, "dev", [(i, (i + k) % dev_count) for i in range(dev_count)]))
            pieces = jnp.concatenate(blocks, axis=0)
            shifted = ((me - owner) % dev_count) * slot_count + slot_of
            picked = jnp.take(pieces, shifted, axis=0, mode="clip")
        else:
            pieces = lax.all_to_all(rounded, "dev", split_axis=1, concat_axis=0, tiled=True)
            picked = jnp.take(pieces, target, axis=0, mode="clip")
        gathered = lax.all_gather(picked, "rep", axis=2, tiled=True)
        if c == 0:
            late_inputs = lax.optimization_barrier((start_rows, momentum_rows, changes[0], changes[1], coeffs, gathered))
            gathered = late_inputs[5]
        returned = place_half(gathered, width, c, returned)
    late_start, late_momentum, late_change0, late_change1, late_coeffs, _ = late_inputs
    coeffs = late_coeffs
    fresh_start, fresh_momentum = fresh(late_start, late_momentum, jnp.concatenate([late_change0, late_change1], axis=2), basis_part)
    new_momentum = jnp.where(owned_mask, fresh_momentum, late_momentum)
    new_start = jnp.where(owned_mask, fresh_start, late_start)
    vec_change = vec_start - vec_summed / rep_count
    vec_new_momentum = outer_momentum * vec_momentum + vec_change
    vec_new = vec_start - outer_rate * (vec_change + outer_momentum * vec_new_momentum)
    return (new_start[None], new_momentum[None], returned, vec_new, vec_new_momentum)


def solution(mesh):
    return jax.shard_map(
        body,
        mesh=mesh,
        in_specs=(
            P("rep", None, "dev", None),
            P(),
            P("dev", None, None, "rep"),
            P("dev", None, None, "rep"),
            P(),
            P("rep", None, None),
            P(),
            P(),
        ),
        out_specs=(
            P("dev", None, None, "rep"),
            P("dev", None, None, "rep"),
            P(None, "dev", None),
            P(),
            P(),
        ),
        check_vma=False,
    )
```

```python
import jax
import jax.numpy as jnp
from jax import lax
from jax.sharding import PartitionSpec as P
from jax.experimental import pallas as pl

EMB_FIRST = 96


outer_rate = 0.7
outer_momentum = 0.9


def rep_sum(x):
    rep_count = lax.axis_size("rep")
    if rep_count != 4:
        total = x.astype(jnp.bfloat16)
        step = 1
        while step < rep_count:
            other = lax.ppermute(total, "rep", [(i, i ^ step) for i in range(rep_count)])
            total = total.astype(jnp.float32) + other.astype(jnp.float32)
            step *= 2
            if step < rep_count:
                total = total.astype(jnp.bfloat16)
        return total
    core = lax.axis_index("rep") % 2
    mine = x.astype(jnp.bfloat16)
    other = lax.ppermute(mine, "rep", [(i, i ^ 1) for i in range(4)])
    pair = (mine.astype(jnp.float32) + other.astype(jnp.float32)).astype(jnp.bfloat16)
    pair = pair.reshape((2, x.shape[0] // 2) + x.shape[1:])
    part = lax.dynamic_index_in_dim(pair, core, 0, keepdims=False)
    across = lax.ppermute(part, "rep", [(i, i ^ 2) for i in range(4)])
    done = part.astype(jnp.float32) + across.astype(jnp.float32)
    rest = lax.ppermute(done, "rep", [(i, i ^ 1) for i in range(4)])
    first = jnp.where(core == 0, done, rest)
    second = jnp.where(core == 0, rest, done)
    return jnp.concatenate([first, second], axis=0)


def _copy_kernel(x_ref, o_ref):
    o_ref[...] = x_ref[...].reshape(o_ref.shape)


def take_half(x, width, half):
    units, rows, full = x.shape
    quarters = full // (2 * width)
    return pl.pallas_call(
        _copy_kernel,
        grid=(quarters,),
        in_specs=[pl.BlockSpec((units, rows, width), lambda q: (0, 0, 2 * q + half))],
        out_specs=pl.BlockSpec((1, units, rows, width), lambda q: (q, 0, 0, 0)),
        out_shape=jax.ShapeDtypeStruct((quarters, units, rows, width), x.dtype),
    )(x)


def _place_kernel(a_ref, base_ref, o_ref):
    del base_ref
    o_ref[...] = a_ref[...]


def place_half(a, width, half, base=None):
    units, rows, part = a.shape
    quarters = part // width
    in_spec = pl.BlockSpec((units, rows, width), lambda q: (0, 0, q))
    out_spec = pl.BlockSpec((units, rows, width), lambda q: (0, 0, 2 * q + half))
    out_shape = jax.ShapeDtypeStruct((units, rows, 2 * part), a.dtype)
    if base is None:
        return pl.pallas_call(
            _copy_kernel, grid=(quarters,), in_specs=[in_spec], out_specs=out_spec, out_shape=out_shape
        )(a)
    return pl.pallas_call(
        _place_kernel,
        grid=(quarters,),
        in_specs=[in_spec, pl.BlockSpec(memory_space=pl.ANY)],
        out_specs=out_spec,
        out_shape=out_shape,
        input_output_aliases={1: 0},
    )(a, base)


def body(group_weights, owner, start_weights, momentum, basis, vec_groups, vec_start, vec_momentum):
    dev_count = lax.axis_size("dev")
    rep_count = lax.axis_size("rep")
    unit_count = owner.shape[0]
    slot_count = start_weights.shape[1]
    quarter = start_weights.shape[3]
    unit_ids = jnp.arange(unit_count, dtype=jnp.int32)
    same_owner = owner[:, None] == owner[None, :]
    earlier = unit_ids[None, :] < unit_ids[:, None]
    slot_of = jnp.sum((same_owner & earlier).astype(jnp.int32), axis=1)
    target = owner * slot_count + slot_of
    positions = jnp.arange(dev_count * slot_count, dtype=jnp.int32)
    placed = target[:, None] == positions[None, :]
    source_unit = jnp.sum(jnp.where(placed, unit_ids[:, None], 0), axis=0)
    own_rows = group_weights[0]
    width = quarter // 2
    start_rows = start_weights[0]
    momentum_rows = momentum[0]
    my_slots = lax.axis_index("dev") * slot_count + jnp.arange(slot_count, dtype=jnp.int32)
    own_placed = target[:, None] == my_slots[None, :]
    is_owned = jnp.any(own_placed, axis=0)
    is_embedding = jnp.any(own_placed & (unit_ids >= EMB_FIRST)[:, None], axis=0)
    first_column = lax.axis_index("rep") * quarter
    basis_part = lax.dynamic_slice_in_dim(basis, first_column, quarter, 1)
    halves = [slice(c * width, (c + 1) * width) for c in range(2)]
    held = start_rows - (outer_rate * outer_momentum * outer_momentum) * momentum_rows
    changes = []
    coeff_terms = None
    for c in range(2):
        half = take_half(own_rows, width, c)
        summed = lax.psum_scatter(half, "rep", scatter_dimension=0, tiled=True)[0]
        if c == 1 and dev_count <= 8:
            me = lax.axis_index("dev")
            part_rows = summed.shape[1]
            arrived = jnp.zeros((slot_count, dev_count * part_rows, width), summed.dtype)
            picked = jnp.take(summed, source_unit, axis=0, mode="clip").reshape(dev_count, slot_count, part_rows, width)
            for k in range(dev_count):
                block = lax.dynamic_index_in_dim(picked, (me + k) % dev_count, 0, keepdims=False)
                if k:
                    block = lax.ppermute(block, "dev", [(i, (i + k) % dev_count) for i in range(dev_count)])
                if k == 1:
                    coeff_terms, block = lax.optimization_barrier((coeff_terms, block))
                arrived = lax.dynamic_update_slice_in_dim(arrived, block, ((me - k) % dev_count) * part_rows, 1)
        else:
            picked = jnp.take(summed, source_unit, axis=0, mode="clip")
            arrived = lax.all_to_all(
                picked.reshape(dev_count, slot_count, summed.shape[1], summed.shape[2]),
                "dev",
                split_axis=0,
                concat_axis=2,
                tiled=True,
            )[0]
        change = start_rows[:, :, halves[c]] - arrived.astype(jnp.float32) / rep_count
        changes.append(change)
        term = jnp.einsum("sbq,kq->skb", change, basis_part[:, halves[c]], precision=lax.Precision.HIGH)
        coeff_terms = term if coeff_terms is None else coeff_terms + term
    rank = coeff_terms.shape[1]
    rows_all = coeff_terms.shape[2]
    vec_terms = vec_groups[0]
    vec_rows = vec_terms.shape[0]
    vec_padded = jnp.pad(vec_terms, ((0, (-vec_rows) % 16), (0, 0)))
    coeff_block = coeff_terms.astype(jnp.bfloat16).reshape(slot_count * rank, rows_all)
    vec_block = vec_padded.reshape(-1, rows_all)
    joined = rep_sum(jnp.concatenate([coeff_block, vec_block], axis=0))
    coeffs = joined[: slot_count * rank].reshape(slot_count, rank, rows_all)
    vec_summed = joined[slot_count * rank:].reshape(vec_padded.shape)[:vec_rows]
    owned_mask = is_owned[:, None, None]
    emb_mask = is_embedding[:, None, None]

    def fresh(start_part, momentum_part, change, basis_cols):
        projected = jnp.einsum("skb,kq->sbq", coeffs, basis_cols, precision=lax.Precision.HIGH)
        outer_grad = jnp.where(emb_mask, projected, change)
        fresh_momentum = outer_momentum * momentum_part + outer_grad
        fresh_start = start_part - outer_rate * (outer_grad + outer_momentum * fresh_momentum)
        return fresh_start, fresh_momentum

    returned = None
    all_changes = jnp.concatenate(changes, axis=2)
    projected_all = jnp.einsum("skb,kq->sbq", coeffs, basis_part, precision=lax.Precision.HIGH)
    grad_all = jnp.where(emb_mask, projected_all, all_changes)
    rounded_all = (held - (outer_rate * (1.0 + outer_momentum)) * grad_all).astype(jnp.bfloat16)
    for c in range(2):
        rounded = rounded_all[:, :, halves[c]]
        if dev_count <= 8:
            me = lax.axis_index("dev")
            part_rows = rounded.shape[1] // dev_count
            blocks = [lax.dynamic_slice_in_dim(rounded, me * part_rows, part_rows, 1)]
            for k in range(1, dev_count):
                out_rows = lax.dynamic_slice_in_dim(rounded, ((me + k) % dev_count) * part_rows, part_rows, 1)
                blocks.append(lax.ppermute(out_rows, "dev", [(i, (i + k) % dev_count) for i in range(dev_count)]))
            pieces = jnp.concatenate(blocks, axis=0)
            shifted = ((me - owner) % dev_count) * slot_count + slot_of
            picked = jnp.take(pieces, shifted, axis=0, mode="clip")
        else:
            pieces = lax.all_to_all(rounded, "dev", split_axis=1, concat_axis=0, tiled=True)
            picked = jnp.take(pieces, target, axis=0, mode="clip")
        gathered = lax.all_gather(picked, "rep", axis=2, tiled=True)
        if c == 0:
            late_inputs = lax.optimization_barrier((start_rows, momentum_rows, changes[0], changes[1], coeffs, gathered))
            gathered = late_inputs[5]
        returned = place_half(gathered, width, c, returned)
    late_start, late_momentum, late_change0, late_change1, late_coeffs, _ = late_inputs
    coeffs = late_coeffs
    fresh_start, fresh_momentum = fresh(late_start, late_momentum, jnp.concatenate([late_change0, late_change1], axis=2), basis_part)
    new_momentum = jnp.where(owned_mask, fresh_momentum, late_momentum)
    new_start = jnp.where(owned_mask, fresh_start, late_start)
    vec_change = vec_start - vec_summed / rep_count
    vec_new_momentum = outer_momentum * vec_momentum + vec_change
    vec_new = vec_start - outer_rate * (vec_change + outer_momentum * vec_new_momentum)
    return (new_start[None], new_momentum[None], returned, vec_new, vec_new_momentum)


def solution(mesh):
    return jax.shard_map(
        body,
        mesh=mesh,
        in_specs=(
            P("rep", None, "dev", None),
            P(),
            P("dev", None, None, "rep"),
            P("dev", None, None, "rep"),
            P(),
            P("rep", None, None),
            P(),
            P(),
        ),
        out_specs=(
            P("dev", None, None, "rep"),
            P("dev", None, None, "rep"),
            P(None, "dev", None),
            P(),
            P(),
        ),
        check_vma=False,
    )
```
